512 devices in a mesh: band: 32 (over x, y), seq: 16 (over z, core).
Axes of the slice: x: 4, y: 8, z: 8, core: 2. Of those that a mesh axis runs over, the one named last changes fastest.
Arguments:
- posteriors: bfloat16 [32, 262144], P(None, ('band', 'seq'))
- seed_mask: int32 [262144], P(('band', 'seq')), may hold values 0 or 1
- frame_perm: int32 [512, 512], P(('band', 'seq')), may hold values from 0 to 511, each once within a row
- lengths: int32 [256], replicated, may hold values from 1 to 4096, 262144 in all
- embeddings: bfloat16 [262144, 256], P(('band', 'seq')), may hold values from -12 to 12
- partners: int32 [2048, 32], P(('band', 'seq')), may hold values from 0 to 127, as said below
- levels: int32 [2048, 32], P(('band', 'seq')), may hold values from 1 to 8, as said below
Outputs:
- spread_labels: float32 [32, 262144], P(None, ('band', 'seq'))
The draws below stay inside these ranges and needn't reach their ends.
Inputs may be any that keep to these rules, and one draw needn't show every extreme that they name: `partners`: within each seq index s, slot k pairs the 128 tiles mutually: if tile number a names b in slot k then b names a in slot k; no tile names itself. `levels`: two tiles paired in slot k carry the same level.
All inputs are finite; a program needn't handle non-finite values. No bound on the sum of `seed_mask` on one device may be relied on, other than what follows from the above.
Results may differ from the reference program's by a relative error of at most 0.007.
Values may be sent and summed in bfloat16 or wider, within the bound.
No kernel may reach another device: no remote copies, remote signals or barrier semaphores. Data moves between devices by JAX's collectives and lax.ppermute only.
A program may use at most 64 MiB of HBM per device.

```python
import math
import jax
import jax.numpy as jnp
import numpy as np
from jax import lax

LABELS = 32
EMBED = 256
TILE_DEV = 4
NEIGHBORS = 32
RADIUS = 64
ITERS = 3
MAXLEN = 4096
FRAMES_DEV = 512
FRAMES = 262144
TILES = 2048
GROUP_TILES = 128
SEQ_GROUPS = 16
SLOT = 16
UTTS = 256
N_SEQ = 16
DEVICES = 512


def draw_posteriors(key, part):
    base = jax.random.uniform(jax.random.fold_in(key, 3), (LABELS, FRAMES), jnp.float32, 0.05, 1.0)
    frame_at = jnp.arange(FRAMES, dtype=jnp.int32)
    shard_seq = frame_at // FRAMES_DEV % SEQ_GROUPS
    rising = 1.0 + 2.0 * shard_seq.astype(jnp.float32) / max(SEQ_GROUPS - 1, 1)
    values = base * rising[None, :]
    return values.astype(jnp.bfloat16)


def pairing(key):
    count = SEQ_GROUPS * NEIGHBORS
    keys = jax.random.split(jax.random.fold_in(key, 7), count)
    orders = jax.vmap(lambda one_key: jax.random.permutation(one_key, jnp.arange(GROUP_TILES, dtype=jnp.int32)))(keys)
    inverse = jnp.argsort(orders, axis=1).astype(jnp.int32)
    mates = jnp.take_along_axis(orders, jnp.bitwise_xor(inverse, 1), axis=1)
    pair_level = jax.random.randint(jax.random.fold_in(key, 11), (count, GROUP_TILES // 2), 1, 9, jnp.int32)
    grade = jnp.take_along_axis(pair_level, inverse // 2, axis=1)
    band_count = GROUP_TILES // TILE_DEV

    def arrange(table):
        table = table.reshape(SEQ_GROUPS, NEIGHBORS, GROUP_TILES)
        table = jnp.transpose(table, (0, 2, 1)).reshape(SEQ_GROUPS, band_count, TILE_DEV, NEIGHBORS)
        return jnp.transpose(table, (1, 0, 2, 3)).reshape(TILES, NEIGHBORS)
    return (arrange(mates), arrange(grade))


def draw_partners(key, part):
    return pairing(key)[0]


def draw_levels(key, part):
    return pairing(key)[1]


def set_ends(drawn, rng, least, top_value):
    longest = drawn.shape.index(max(drawn.shape))
    spots = []
    for shift in (0, 1):
        where = [jax.random.randint(jax.random.fold_in(rng, axis), (), 0, length) for axis, length in enumerate(drawn.shape)]
        where[longest] = (where[longest] + shift) % drawn.shape[longest]
        spots.append(tuple(where))
    return drawn.at[spots[0]].set(least).at[spots[1]].set(top_value)


def block_levels(rng, shape, shards, low, top_value):
    loudness = 1.0
    for dim, parts in shards:
        heights = jax.random.uniform(jax.random.fold_in(jax.random.fold_in(rng, 6), dim), (parts,), jnp.float32, low / len(shards), top_value / len(shards))
        loudness = loudness * jnp.repeat(jnp.exp(heights), shape[dim] // parts).reshape((-1,) + (1,) * (len(shape) - 1 - dim))
    return loudness


def profile(number_of, total, reach, lean):
    loads = [(1 << 20) // math.isqrt(standing ** lean) + 1 for standing in range(2, number_of + 1)]
    spare, counts = total - reach - (number_of - 1), [1] * (number_of - 1)
    while spare > 0:
        movable = [i for i in range(number_of - 1) if counts[i] < reach]
        pool, left = sum([loads[i] for i in movable]), spare
        for i in movable:
            more = min(reach - counts[i], max(1, left * loads[i] // pool), spare)
            counts[i] = counts[i] + more
            spare = spare - more
    return np.array([reach] + counts)


def uneven_parts(stream_key, count, total, most, slope):
    if count == 2:
        one = jax.random.randint(stream_key, (), max(1, total - most), min(most, total - 1) + 1)
        return jnp.stack([one, total - one])
    sizes = jnp.asarray(profile(count, total, most, slope), jnp.int32)
    pairs = (count - 1) // 2
    donor, sink = sizes[1:1 + 2 * pairs:2], sizes[2:2 + 2 * pairs:2]
    slack = jnp.minimum(donor - 1, most - sink)
    passed = jax.random.randint(jax.random.fold_in(stream_key, 1), (pairs,), 0, 1 << 20) % (slack + 1)
    sizes = sizes.at[1:1 + 2 * pairs:2].set(donor - passed).at[2:2 + 2 * pairs:2].set(sink + passed)
    return sizes[jax.random.permutation(jax.random.fold_in(stream_key, 2), count)]


def centred(rng, extent, width, bound, pieces=(), kind=jnp.bfloat16):
    array = jax.random.normal(rng, extent, jnp.float32) * width
    if len(pieces) > 0:
        array = block_levels(rng, extent, pieces, -0.22, 0.18) * array
    return jnp.clip(array, min=-bound, max=bound).astype(kind)


def setup_inputs(seed: int = 0) -> dict:
    arg_keys = jax.random.split(jax.random.key(seed), 8)
    return {
        "posteriors": draw_posteriors(jax.random.fold_in(arg_keys[7], 71), 0),
        "seed_mask": set_ends((jax.random.randint(arg_keys[1], (FRAMES,), 0, 4) < 1).astype(jnp.int32), jax.random.fold_in(arg_keys[1], 1), 0, 1),
        "frame_perm": jax.vmap(lambda own: jax.random.permutation(own, FRAMES_DEV))(jax.random.split(arg_keys[2], DEVICES)).reshape((DEVICES, FRAMES_DEV)).astype(jnp.int32),
        "lengths": uneven_parts(arg_keys[3], UTTS, FRAMES, MAXLEN, 2).astype(jnp.int32),
        "embeddings": centred(arg_keys[4], (FRAMES, EMBED), 2.0, 12.0, ((0, 512),)),
        "partners": draw_partners(jax.random.fold_in(arg_keys[7], 71), 0),
        "levels": draw_levels(jax.random.fold_in(arg_keys[7], 71), 0),
    }


decay_len = 16.0
spread_rate = 0.9

def temporal_apply(values, seg):
    frame_at = jnp.arange(FRAMES, dtype=jnp.int32)

    def add_offset(dist, acc):
        weight = jnp.exp(-dist.astype(jnp.float32) / decay_len).astype(jnp.bfloat16)
        weight = lax.optimization_barrier(weight).astype(jnp.float32)
        ahead = (frame_at + dist < FRAMES) & (jnp.roll(seg, -dist) == seg)
        behind = (frame_at - dist >= 0) & (jnp.roll(seg, dist) == seg)
        front = jnp.where(ahead[None, :], jnp.roll(values, -dist, axis=1), jnp.float32(0.0))
        back = jnp.where(behind[None, :], jnp.roll(values, dist, axis=1), jnp.float32(0.0))
        return acc + weight * (front + back)
    return lax.fori_loop(1, RADIUS + 1, add_offset, jnp.zeros(values.shape, jnp.float32))

def affinity_block(device, embeddings, partners, levels):
    own_rows = lax.dynamic_slice_in_dim(embeddings, (device * FRAMES_DEV).astype(jnp.int32), FRAMES_DEV, 0)
    own_rows = own_rows.reshape(TILE_DEV, 128, EMBED)
    slots = lax.dynamic_slice_in_dim(partners, (device * TILE_DEV).astype(jnp.int32), TILE_DEV, 0)
    grade = lax.dynamic_slice_in_dim(levels, (device * TILE_DEV).astype(jnp.int32), TILE_DEV, 0)
    group = device % N_SEQ
    target = (slots // TILE_DEV * N_SEQ + group) * TILE_DEV + slots % TILE_DEV
    partner_rows = embeddings.reshape(TILES, 128, EMBED)[target]
    inner_prod = jnp.einsum('tkje,tie->tkji', partner_rows.astype(jnp.float32), own_rows.astype(jnp.float32))
    weight = jnp.exp(0.5 * (inner_prod / math.sqrt(EMBED))) * (grade.astype(jnp.float32) / 8.0)[:, :, None, None] / 128.0
    return (weight.astype(jnp.bfloat16), target)

def reference(posteriors, seed_mask, frame_perm, lengths, embeddings, partners, levels):
    dev_ids = jnp.arange(DEVICES, dtype=jnp.int32)[:, None]
    column = jnp.arange(FRAMES_DEV, dtype=jnp.int32)[None, :]
    source = dev_ids * FRAMES_DEV + frame_perm
    target = (column // SLOT * N_SEQ + dev_ids % N_SEQ) * FRAMES_DEV + dev_ids // N_SEQ * SLOT + column % SLOT
    seeded = posteriors * seed_mask.astype(jnp.bfloat16)[None, :]
    labels = jnp.zeros((LABELS, FRAMES), jnp.float32)
    labels = labels.at[:, target.reshape(-1)].set(seeded[:, source.reshape(-1)].astype(jnp.float32))
    utt_ends = jnp.cumsum(lengths)
    seg = jnp.searchsorted(utt_ends, jnp.arange(FRAMES, dtype=jnp.int32), side='right').astype(jnp.int32)
    device_list = jnp.arange(DEVICES, dtype=jnp.int32)

    def knn_degree(device):
        weight, target_tiles = affinity_block(device, embeddings, partners, levels)
        return lax.optimization_barrier(jnp.sum(weight.astype(jnp.float32), axis=(1, 2)))
    far_degree = lax.map(knn_degree, device_list).reshape(FRAMES)
    near_degree = temporal_apply(jnp.ones((1, FRAMES), jnp.float32), seg)[0]
    degree = near_degree + far_degree
    norm_scale = 1.0 / jnp.sqrt(degree)

    def operate(field):
        lifted = (norm_scale[None, :] * field).astype(jnp.bfloat16)
        near_term = temporal_apply(lifted.astype(jnp.float32), seg)
        tiled = lifted.reshape(LABELS, TILES, 128)

        def knn_apply(device):
            weight, target_tiles = affinity_block(device, embeddings, partners, levels)
            picked = tiled[:, target_tiles].astype(jnp.float32)
            return jnp.einsum('ctkj,tkji->cti', picked, weight.astype(jnp.float32))
        far_term = lax.map(knn_apply, device_list)
        far_term = jnp.transpose(far_term, (1, 0, 2, 3)).reshape(LABELS, FRAMES)
        return field - spread_rate * norm_scale[None, :] * (near_term + far_term)
    solution = jnp.zeros((LABELS, FRAMES), jnp.float32)
    residual = labels
    direction = labels
    norm_now = lax.optimization_barrier(jnp.sum(residual * residual, axis=1))
    for iteration in range(ITERS):
        image = operate(direction)
        alpha = norm_now / lax.optimization_barrier(jnp.sum(direction * image, axis=1))
        solution = solution + alpha[:, None] * direction
        residual = residual - alpha[:, None] * image
        norm_next = lax.optimization_barrier(jnp.sum(residual * residual, axis=1))
        direction = residual + (norm_next / norm_now)[:, None] * direction
        norm_now = norm_next
    return solution
```

```python
import math

import jax
import jax.numpy as jnp
from jax import lax
from jax.sharding import PartitionSpec as P

RADIUS = 64
ITERS = 3


decay_len = 16.0
spread_rate = 0.9


def with_halo(cells, sides, width):
    for axis, dim in sides:
        count = lax.axis_size(axis)
        ends = count - 1
        head = lax.slice_in_dim(cells, 0, width, axis=dim)
        tail = lax.slice_in_dim(cells, cells.shape[dim] - width, cells.shape[dim], axis=dim)
        cells = jnp.concatenate(
            [
                lax.ppermute(tail, axis, [(i, (i + 1) % count) for i in range(ends)]),
                cells,
                lax.ppermute(head, axis, [((i + 1) % count, i) for i in range(ends)]),
            ],
            axis=dim,
        )
    return cells


def butterfly_sum(values):
    count = lax.axis_size("band") * lax.axis_size("seq")
    for bit in range(count.bit_length() - 1):
        step = 1 << bit
        values = values + lax.ppermute(
            values, ("band", "seq"), [(i, i ^ step) for i in range(count)]
        )
    return values


def band_exchange(block):
    count = lax.axis_size("band")
    bits = count.bit_length() - 1
    me = lax.axis_index("band")
    held = block[None]
    for bit in reversed(range(bits)):
        step = 1 << bit
        other = lax.ppermute(held, "band", [(i, i ^ step) for i in range(count)])
        low = ((me >> bit) & 1) == 0
        held = jnp.where(
            low,
            jnp.concatenate([held, other], axis=0),
            jnp.concatenate([other, held], axis=0),
        )
    return held


def bit_reverse(values, bits):
    out = jnp.zeros_like(values)
    for bit in range(bits):
        out = out | (((values >> bit) & 1) << (bits - 1 - bit))
    return out


def on_device(posteriors, seed_mask, frame_perm, lengths, embeddings, partners, levels):
    channels, frames = posteriors.shape
    band_count = lax.axis_size("band")
    groups = lax.axis_size("seq")
    tile_count = frames // 128
    seeded = posteriors * seed_mask.astype(jnp.bfloat16)[None, :]
    ordered = jnp.take(seeded, frame_perm[0], axis=1).reshape(
        channels, band_count, frames // band_count
    )
    arrived = lax.all_to_all(ordered, "band", split_axis=1, concat_axis=1, tiled=True)
    labels = arrived.reshape(channels, frames).astype(jnp.float32)
    device = lax.axis_index("band") * groups + lax.axis_index("seq")
    frame_total = frames * band_count * groups
    window = 128 + 2 * RADIUS
    global_at = device * frames - RADIUS + jnp.arange(frames + 2 * RADIUS, dtype=jnp.int32)
    utt_ends = jnp.cumsum(lengths)
    owner_seg = jnp.sum((utt_ends[None, :] <= global_at[:, None]).astype(jnp.int32), axis=1)
    inside = (global_at >= 0) & (global_at < frame_total)
    tile_off = (jnp.arange(tile_count, dtype=jnp.int32) * 128)[:, None, None]
    win_pos = tile_off + jnp.arange(window, dtype=jnp.int32)[None, :, None]
    row_pos = tile_off + RADIUS + jnp.arange(128, dtype=jnp.int32)[None, None, :]
    offset = jnp.abs(win_pos - row_pos)
    linked = (
        (offset >= 1)
        & (offset <= RADIUS)
        & (owner_seg[win_pos] == owner_seg[row_pos])
        & inside[win_pos]
    )
    band_tiles = jnp.where(
        linked, jnp.exp(-offset.astype(jnp.float32) / decay_len), jnp.float32(0.0)
    ).astype(jnp.bfloat16)
    near_degree = jnp.sum(band_tiles.astype(jnp.float32), axis=1).reshape(frames)
    gathered = lax.all_gather(embeddings, "band", axis=0, tiled=True)
    embed_width = embeddings.shape[1]
    partner_rows = gathered.reshape(-1, 128, embed_width)[partners]
    own_rows = embeddings.reshape(tile_count, 128, embed_width)
    inner_prod = jnp.einsum(
        "tkje,tie->tkji", partner_rows, own_rows, preferred_element_type=jnp.float32
    )
    affinity = (
        jnp.exp(0.5 * (inner_prod / math.sqrt(embed_width)))
        * (levels.astype(jnp.float32) / 8.0)[:, :, None, None]
        / 128.0
    )
    affinity = affinity.astype(jnp.bfloat16)
    far_degree = jnp.sum(affinity.astype(jnp.float32), axis=(1, 2)).reshape(frames)
    norm_scale = 1.0 / jnp.sqrt(near_degree + far_degree)

    per_band = frames // 128
    band_bits = band_count.bit_length() - 1
    held_partners = bit_reverse(partners // per_band, band_bits) * per_band + partners % per_band

    def squares(residual):
        return butterfly_sum(jnp.sum(residual * residual, axis=1))

    solution = jnp.zeros((channels, frames), jnp.float32)
    residual = labels
    direction = labels
    norm_now = squares(residual)
    for iteration in range(ITERS):
        lifted = (norm_scale[None, :] * direction).astype(jnp.bfloat16)
        padded = with_halo(lifted, ((("band", "seq"), 1),), RADIUS)
        windows = jnp.stack(
            [padded[:, position * 128 : position * 128 + window] for position in range(tile_count)],
            axis=0,
        )
        near_term = jnp.einsum(
            "tcw,twa->cta", windows, band_tiles, preferred_element_type=jnp.float32
        ).reshape(channels, frames)
        held = band_exchange(lifted).reshape(band_count, channels, -1, 128)
        spread = jnp.transpose(held, (1, 0, 2, 3)).reshape(channels, -1, 128)
        far_tiles = spread[:, held_partners]
        far_term = jnp.einsum(
            "ctkj,tkji->cti", far_tiles, affinity, preferred_element_type=jnp.float32
        ).reshape(channels, frames)
        image = direction - spread_rate * norm_scale[None, :] * (near_term + far_term)
        curve = butterfly_sum(jnp.sum(direction * image, axis=1))
        alpha = norm_now / curve
        solution = solution + alpha[:, None] * direction
        residual = residual - alpha[:, None] * image
        norm_next = squares(residual)
        direction = residual + (norm_next / norm_now)[:, None] * direction
        norm_now = norm_next
    return solution


def solution(mesh):
    placed = (
        P(None, ("band", "seq")),
        P(("band", "seq")),
        P(("band", "seq"), None),
        P(),
        P(("band", "seq"), None),
        P(("band", "seq"), None),
        P(("band", "seq"), None),
    )
    return jax.shard_map(
        on_device, mesh=mesh, in_specs=placed, out_specs=P(None, ("band", "seq")), check_vma=False
    )
```

```python
import math

import jax
import jax.numpy as jnp
from jax import lax
from jax.sharding import PartitionSpec as P

RADIUS = 64
ITERS = 3


decay_len = 16.0
spread_rate = 0.9


def with_halo(cells, sides, width):
    for axis, dim in sides:
        count = lax.axis_size(axis)
        ends = count - 1
        head = lax.slice_in_dim(cells, 0, width, axis=dim)
        tail = lax.slice_in_dim(cells, cells.shape[dim] - width, cells.shape[dim], axis=dim)
        cells = jnp.concatenate(
            [
                lax.ppermute(tail, axis, [(i, (i + 1) % count) for i in range(ends)]),
                cells,
                lax.ppermute(head, axis, [((i + 1) % count, i) for i in range(ends)]),
            ],
            axis=dim,
        )
    return cells


def total_over_devices(values):
    count = lax.axis_size("band") * lax.axis_size("seq")
    spread = jnp.broadcast_to(values[None], (count,) + values.shape)
    rows = lax.all_to_all(spread, ("band", "seq"), split_axis=0, concat_axis=0, tiled=True)
    return jnp.sum(rows, axis=0)


def band_gather(block):
    count = lax.axis_size("band")
    spread = jnp.broadcast_to(block[None], (count,) + block.shape)
    return lax.all_to_all(spread, "band", split_axis=0, concat_axis=0, tiled=True)


def on_device(posteriors, seed_mask, frame_perm, lengths, embeddings, partners, levels):
    channels, frames = posteriors.shape
    band_count = lax.axis_size("band")
    groups = lax.axis_size("seq")
    tile_count = frames // 128
    seeded = posteriors * seed_mask.astype(jnp.bfloat16)[None, :]
    ordered = jnp.take(seeded, frame_perm[0], axis=1).reshape(
        channels, band_count, frames // band_count
    )
    arrived = lax.all_to_all(ordered, "band", split_axis=1, concat_axis=1, tiled=True)
    labels = arrived.reshape(channels, frames).astype(jnp.float32)
    device = lax.axis_index("band") * groups + lax.axis_index("seq")
    frame_total = frames * band_count * groups
    window = 128 + 2 * RADIUS
    global_at = device * frames - RADIUS + jnp.arange(frames + 2 * RADIUS, dtype=jnp.int32)
    utt_ends = jnp.cumsum(lengths)
    owner_seg = jnp.sum((utt_ends[None, :] <= global_at[:, None]).astype(jnp.int32), axis=1)
    inside = (global_at >= 0) & (global_at < frame_total)
    tile_off = (jnp.arange(tile_count, dtype=jnp.int32) * 128)[:, None, None]
    win_pos = tile_off + jnp.arange(window, dtype=jnp.int32)[None, :, None]
    row_pos = tile_off + RADIUS + jnp.arange(128, dtype=jnp.int32)[None, None, :]
    offset = jnp.abs(win_pos - row_pos)
    linked = (
        (offset >= 1)
        & (offset <= RADIUS)
        & (owner_seg[win_pos] == owner_seg[row_pos])
        & inside[win_pos]
    )
    band_tiles = jnp.where(
        linked, jnp.exp(-offset.astype(jnp.float32) / decay_len), jnp.float32(0.0)
    ).astype(jnp.bfloat16)
    near_degree = jnp.sum(band_tiles.astype(jnp.float32), axis=1).reshape(frames)
    gathered = band_gather(embeddings)
    embed_width = embeddings.shape[1]
    partner_rows = gathered.reshape(-1, 128, embed_width)[partners]
    own_rows = embeddings.reshape(tile_count, 128, embed_width)
    inner_prod = jnp.einsum(
        "tkje,tie->tkji", partner_rows, own_rows, preferred_element_type=jnp.float32
    )
    affinity = (
        jnp.exp(0.5 * (inner_prod / math.sqrt(embed_width)))
        * (levels.astype(jnp.float32) / 8.0)[:, :, None, None]
        / 128.0
    )
    affinity = affinity.astype(jnp.bfloat16)
    far_degree = jnp.sum(affinity.astype(jnp.float32), axis=(1, 2)).reshape(frames)
    norm_scale = 1.0 / jnp.sqrt(near_degree + far_degree)

    def squares(residual):
        return total_over_devices(jnp.sum(residual * residual, axis=1))

    solution = jnp.zeros((channels, frames), jnp.float32)
    residual = labels
    direction = labels
    first_norm = jnp.sum(residual * residual, axis=1)
    for iteration in range(ITERS):
        lifted = (norm_scale[None, :] * direction).astype(jnp.bfloat16)
        padded = with_halo(lifted, ((("band", "seq"), 1),), RADIUS)
        windows = jnp.stack(
            [padded[:, position * 128 : position * 128 + window] for position in range(tile_count)],
            axis=0,
        )
        near_term = jnp.einsum(
            "tcw,twa->cta", windows, band_tiles, preferred_element_type=jnp.float32
        ).reshape(channels, frames)
        spread = jnp.transpose(band_gather(lifted), (1, 0, 2)).reshape(channels, -1, 128)
        far_tiles = spread[:, partners]
        far_term = jnp.einsum(
            "ctkj,tkji->cti", far_tiles, affinity, preferred_element_type=jnp.float32
        ).reshape(channels, frames)
        image = direction - spread_rate * norm_scale[None, :] * (near_term + far_term)
        curve = jnp.sum(direction * image, axis=1)
        if iteration == 0:
            both = total_over_devices(jnp.stack([first_norm, curve]))
            norm_now, curve = both[0], both[1]
        else:
            curve = total_over_devices(curve)
        alpha = norm_now / curve
        solution = solution + alpha[:, None] * direction
        residual = residual - alpha[:, None] * image
        norm_next = squares(residual)
        direction = residual + (norm_next / norm_now)[:, None] * direction
        norm_now = norm_next
    return solution


def solution(mesh):
    placed = (
        P(None, ("band", "seq")),
        P(("band", "seq")),
        P(("band", "seq"), None),
        P(),
        P(("band", "seq"), None),
        P(("band", "seq"), None),
        P(("band", "seq"), None),
    )
    return jax.shard_map(
        on_device, mesh=mesh, in_specs=placed, out_specs=P(None, ("band", "seq")), check_vma=False
    )
```

```python
import math

import jax
import jax.numpy as jnp
from jax import lax
from jax.sharding import PartitionSpec as P

RADIUS = 64
ITERS = 3


decay_len = 16.0
spread_rate = 0.9


def with_halo(cells, sides, width):
    for axis, dim in sides:
        count = lax.axis_size(axis)
        ends = count - 1
        head = lax.slice_in_dim(cells, 0, width, axis=dim)
        tail = lax.slice_in_dim(cells, cells.shape[dim] - width, cells.shape[dim], axis=dim)
        cells = jnp.concatenate(
            [
                lax.ppermute(tail, axis, [(i, (i + 1) % count) for i in range(ends)]),
                cells,
                lax.ppermute(head, axis, [((i + 1) % count, i) for i in range(ends)]),
            ],
            axis=dim,
        )
    return cells


def total_over_devices(values):
    count = lax.axis_size("band") * lax.axis_size("seq")
    spread = jnp.broadcast_to(values[None], (count,) + values.shape)
    rows = lax.all_to_all(spread, ("band", "seq"), split_axis=0, concat_axis=0, tiled=True)
    return jnp.sum(rows, axis=0)


def band_gather(block):
    count = lax.axis_size("band")
    spread = jnp.broadcast_to(block[None], (count,) + block.shape)
    return lax.all_to_all(spread, "band", split_axis=0, concat_axis=0, tiled=True)


def on_device(posteriors, seed_mask, frame_perm, lengths, embeddings, partners, levels):
    channels, frames = posteriors.shape
    band_count = lax.axis_size("band")
    groups = lax.axis_size("seq")
    tile_count = frames // 128
    seeded = posteriors * seed_mask.astype(jnp.bfloat16)[None, :]
    ordered = jnp.take(seeded, frame_perm[0], axis=1).reshape(
        channels, band_count, frames // band_count
    )
    arrived = lax.all_to_all(ordered, "band", split_axis=1, concat_axis=1, tiled=True)
    labels = arrived.reshape(channels, frames).astype(jnp.float32)
    device = lax.axis_index("band") * groups + lax.axis_index("seq")
    frame_total = frames * band_count * groups
    window = 128 + 2 * RADIUS
    global_at = device * frames - RADIUS + jnp.arange(frames + 2 * RADIUS, dtype=jnp.int32)
    utt_ends = jnp.cumsum(lengths)
    owner_seg = jnp.sum((utt_ends[None, :] <= global_at[:, None]).astype(jnp.int32), axis=1)
    inside = (global_at >= 0) & (global_at < frame_total)
    tile_off = (jnp.arange(tile_count, dtype=jnp.int32) * 128)[:, None, None]
    win_pos = tile_off + jnp.arange(window, dtype=jnp.int32)[None, :, None]
    row_pos = tile_off + RADIUS + jnp.arange(128, dtype=jnp.int32)[None, None, :]
    offset = jnp.abs(win_pos - row_pos)
    linked = (
        (offset >= 1)
        & (offset <= RADIUS)
        & (owner_seg[win_pos] == owner_seg[row_pos])
        & inside[win_pos]
    )
    band_tiles = jnp.where(
        linked, jnp.exp(-offset.astype(jnp.float32) / decay_len), jnp.float32(0.0)
    ).astype(jnp.bfloat16)
    near_degree = jnp.sum(band_tiles.astype(jnp.float32), axis=1).reshape(frames)
    gathered = lax.all_gather(embeddings, "band", axis=0, tiled=True)
    embed_width = embeddings.shape[1]
    partner_rows = gathered.reshape(-1, 128, embed_width)[partners]
    own_rows = embeddings.reshape(tile_count, 128, embed_width)
    inner_prod = jnp.einsum(
        "tkje,tie->tkji", partner_rows, own_rows, preferred_element_type=jnp.float32
    )
    affinity = (
        jnp.exp(0.5 * (inner_prod / math.sqrt(embed_width)))
        * (levels.astype(jnp.float32) / 8.0)[:, :, None, None]
        / 128.0
    )
    affinity = affinity.astype(jnp.bfloat16)
    far_degree = jnp.sum(affinity.astype(jnp.float32), axis=(1, 2)).reshape(frames)
    norm_scale = 1.0 / jnp.sqrt(near_degree + far_degree)

    def squares(residual):
        return total_over_devices(jnp.sum(residual * residual, axis=1))

    solution = jnp.zeros((channels, frames), jnp.float32)
    residual = labels
    direction = labels
    first_norm = jnp.sum(residual * residual, axis=1)
    for iteration in range(ITERS):
        lifted = (norm_scale[None, :] * direction).astype(jnp.bfloat16)
        padded = with_halo(lifted, ((("band", "seq"), 1),), RADIUS)
        windows = jnp.stack(
            [padded[:, position * 128 : position * 128 + window] for position in range(tile_count)],
            axis=0,
        )
        near_term = jnp.einsum(
            "tcw,twa->cta", windows, band_tiles, preferred_element_type=jnp.float32
        ).reshape(channels, frames)
        spread = jnp.transpose(band_gather(lifted), (1, 0, 2)).reshape(channels, -1, 128)
        far_tiles = spread[:, partners]
        far_term = jnp.einsum(
            "ctkj,tkji->cti", far_tiles, affinity, preferred_element_type=jnp.float32
        ).reshape(channels, frames)
        image = direction - spread_rate * norm_scale[None, :] * (near_term + far_term)
        curve = jnp.sum(direction * image, axis=1)
        if iteration == 0:
            both = total_over_devices(jnp.stack([first_norm, curve]))
            norm_now, curve = both[0], both[1]
        else:
            curve = total_over_devices(curve)
        alpha = norm_now / curve
        solution = solution + alpha[:, None] * direction
        residual = residual - alpha[:, None] * image
        norm_next = squares(residual)
        direction = residual + (norm_next / norm_now)[:, None] * direction
        norm_now = norm_next
    return solution


def solution(mesh):
    placed = (
        P(None, ("band", "seq")),
        P(("band", "seq")),
        P(("band", "seq"), None),
        P(),
        P(("band", "seq"), None),
        P(("band", "seq"), None),
        P(("band", "seq"), None),
    )
    return jax.shard_map(
        on_device, mesh=mesh, in_specs=placed, out_specs=P(None, ("band", "seq")), check_vma=False
    )
```

```python
import math

import jax
import jax.numpy as jnp
from jax import lax
from jax.sharding import PartitionSpec as P

RADIUS = 64
ITERS = 3


decay_len = 16.0
spread_rate = 0.9


def with_halo(cells, sides, width):
    for axis, dim in sides:
        count = lax.axis_size(axis)
        ends = count - 1
        head = lax.slice_in_dim(cells, 0, width, axis=dim)
        tail = lax.slice_in_dim(cells, cells.shape[dim] - width, cells.shape[dim], axis=dim)
        cells = jnp.concatenate(
            [
                lax.ppermute(tail, axis, [(i, (i + 1) % count) for i in range(ends)]),
                cells,
                lax.ppermute(head, axis, [((i + 1) % count, i) for i in range(ends)]),
            ],
            axis=dim,
        )
    return cells


def total_over_devices(values):
    for axis in ("seq", "band"):
        count = lax.axis_size(axis)
        spread = jnp.broadcast_to(values[None], (count,) + values.shape)
        rows = lax.all_to_all(spread, axis, split_axis=0, concat_axis=0, tiled=True)
        values = jnp.sum(rows, axis=0)
    return values


def band_gather(block):
    count = lax.axis_size("band")
    spread = jnp.broadcast_to(block[None], (count,) + block.shape)
    return lax.all_to_all(spread, "band", split_axis=0, concat_axis=0, tiled=True)


def on_device(posteriors, seed_mask, frame_perm, lengths, embeddings, partners, levels):
    channels, frames = posteriors.shape
    band_count = lax.axis_size("band")
    groups = lax.axis_size("seq")
    tile_count = frames // 128
    seeded = posteriors * seed_mask.astype(jnp.bfloat16)[None, :]
    ordered = jnp.take(seeded, frame_perm[0], axis=1).reshape(
        channels, band_count, frames // band_count
    )
    arrived = lax.all_to_all(ordered, "band", split_axis=1, concat_axis=1, tiled=True)
    labels = arrived.reshape(channels, frames).astype(jnp.float32)
    device = lax.axis_index("band") * groups + lax.axis_index("seq")
    frame_total = frames * band_count * groups
    window = 128 + 2 * RADIUS
    global_at = device * frames - RADIUS + jnp.arange(frames + 2 * RADIUS, dtype=jnp.int32)
    utt_ends = jnp.cumsum(lengths)
    owner_seg = jnp.sum((utt_ends[None, :] <= global_at[:, None]).astype(jnp.int32), axis=1)
    inside = (global_at >= 0) & (global_at < frame_total)
    tile_off = (jnp.arange(tile_count, dtype=jnp.int32) * 128)[:, None, None]
    win_pos = tile_off + jnp.arange(window, dtype=jnp.int32)[None, :, None]
    row_pos = tile_off + RADIUS + jnp.arange(128, dtype=jnp.int32)[None, None, :]
    offset = jnp.abs(win_pos - row_pos)
    linked = (
        (offset >= 1)
        & (offset <= RADIUS)
        & (owner_seg[win_pos] == owner_seg[row_pos])
        & inside[win_pos]
    )
    band_tiles = jnp.where(
        linked, jnp.exp(-offset.astype(jnp.float32) / decay_len), jnp.float32(0.0)
    ).astype(jnp.bfloat16)
    near_degree = jnp.sum(band_tiles.astype(jnp.float32), axis=1).reshape(frames)
    gathered = lax.all_gather(embeddings, "band", axis=0, tiled=True)
    embed_width = embeddings.shape[1]
    partner_rows = gathered.reshape(-1, 128, embed_width)[partners]
    own_rows = embeddings.reshape(tile_count, 128, embed_width)
    inner_prod = jnp.einsum(
        "tkje,tie->tkji", partner_rows, own_rows, preferred_element_type=jnp.float32
    )
    affinity = (
        jnp.exp(0.5 * (inner_prod / math.sqrt(embed_width)))
        * (levels.astype(jnp.float32) / 8.0)[:, :, None, None]
        / 128.0
    )
    affinity = affinity.astype(jnp.bfloat16)
    far_degree = jnp.sum(affinity.astype(jnp.float32), axis=(1, 2)).reshape(frames)
    norm_scale = 1.0 / jnp.sqrt(near_degree + far_degree)

    def squares(residual):
        return total_over_devices(jnp.sum(residual * residual, axis=1))

    solution = jnp.zeros((channels, frames), jnp.float32)
    residual = labels
    direction = labels
    first_norm = jnp.sum(residual * residual, axis=1)
    for iteration in range(ITERS):
        lifted = (norm_scale[None, :] * direction).astype(jnp.bfloat16)
        padded = with_halo(lifted, ((("band", "seq"), 1),), RADIUS)
        windows = jnp.stack(
            [padded[:, position * 128 : position * 128 + window] for position in range(tile_count)],
            axis=0,
        )
        near_term = jnp.einsum(
            "tcw,twa->cta", windows, band_tiles, preferred_element_type=jnp.float32
        ).reshape(channels, frames)
        spread = jnp.transpose(band_gather(lifted), (1, 0, 2)).reshape(channels, -1, 128)
        far_tiles = spread[:, partners]
        far_term = jnp.einsum(
            "ctkj,tkji->cti", far_tiles, affinity, preferred_element_type=jnp.float32
        ).reshape(channels, frames)
        image = direction - spread_rate * norm_scale[None, :] * (near_term + far_term)
        curve = jnp.sum(direction * image, axis=1)
        if iteration == 0:
            both = total_over_devices(jnp.stack([first_norm, curve]))
            norm_now, curve = both[0], both[1]
        else:
            curve = total_over_devices(curve)
        alpha = norm_now / curve
        solution = solution + alpha[:, None] * direction
        residual = residual - alpha[:, None] * image
        norm_next = squares(residual)
        direction = residual + (norm_next / norm_now)[:, None] * direction
        norm_now = norm_next
    return solution


def solution(mesh):
    placed = (
        P(None, ("band", "seq")),
        P(("band", "seq")),
        P(("band", "seq"), None),
        P(),
        P(("band", "seq"), None),
        P(("band", "seq"), None),
        P(("band", "seq"), None),
    )
    return jax.shard_map(
        on_device, mesh=mesh, in_specs=placed, out_specs=P(None, ("band", "seq")), check_vma=False
    )
```

```python
import math

import jax
import jax.numpy as jnp
from jax import lax
from jax.sharding import PartitionSpec as P

RADIUS = 64
ITERS = 3


decay_len = 16.0
spread_rate = 0.9


def with_halo(cells, sides, width):
    for axis, dim in sides:
        count = lax.axis_size(axis)
        ends = count - 1
        head = lax.slice_in_dim(cells, 0, width, axis=dim)
        tail = lax.slice_in_dim(cells, cells.shape[dim] - width, cells.shape[dim], axis=dim)
        cells = jnp.concatenate(
            [
                lax.ppermute(tail, axis, [(i, (i + 1) % count) for i in range(ends)]),
                cells,
                lax.ppermute(head, axis, [((i + 1) % count, i) for i in range(ends)]),
            ],
            axis=dim,
        )
    return cells


def total_over_devices(values):
    for axis in ("seq", "band"):
        count = lax.axis_size(axis)
        spread = jnp.broadcast_to(values[None], (count,) + values.shape)
        rows = lax.all_to_all(spread, axis, split_axis=0, concat_axis=0, tiled=True)
        values = jnp.sum(rows, axis=0)
    return values


def band_gather(block):
    count = lax.axis_size("band")
    spread = jnp.broadcast_to(block[None], (count,) + block.shape)
    return lax.all_to_all(spread, "band", split_axis=0, concat_axis=0, tiled=True)


def on_device(posteriors, seed_mask, frame_perm, lengths, embeddings, partners, levels):
    channels, frames = posteriors.shape
    band_count = lax.axis_size("band")
    groups = lax.axis_size("seq")
    tile_count = frames // 128
    seeded = posteriors * seed_mask.astype(jnp.bfloat16)[None, :]
    ordered = jnp.take(seeded, frame_perm[0], axis=1).reshape(
        channels, band_count, frames // band_count
    )
    arrived = lax.all_to_all(ordered, "band", split_axis=1, concat_axis=1, tiled=True)
    labels = arrived.reshape(channels, frames).astype(jnp.float32)
    device = lax.axis_index("band") * groups + lax.axis_index("seq")
    frame_total = frames * band_count * groups
    window = 128 + 2 * RADIUS
    global_at = device * frames - RADIUS + jnp.arange(frames + 2 * RADIUS, dtype=jnp.int32)
    utt_ends = jnp.cumsum(lengths)
    owner_seg = jnp.sum((utt_ends[None, :] <= global_at[:, None]).astype(jnp.int32), axis=1)
    inside = (global_at >= 0) & (global_at < frame_total)
    tile_off = (jnp.arange(tile_count, dtype=jnp.int32) * 128)[:, None, None]
    win_pos = tile_off + jnp.arange(window, dtype=jnp.int32)[None, :, None]
    row_pos = tile_off + RADIUS + jnp.arange(128, dtype=jnp.int32)[None, None, :]
    offset = jnp.abs(win_pos - row_pos)
    linked = (
        (offset >= 1)
        & (offset <= RADIUS)
        & (owner_seg[win_pos] == owner_seg[row_pos])
        & inside[win_pos]
    )
    band_tiles = jnp.where(
        linked, jnp.exp(-offset.astype(jnp.float32) / decay_len), jnp.float32(0.0)
    ).astype(jnp.bfloat16)
    near_degree = jnp.sum(band_tiles.astype(jnp.float32), axis=1).reshape(frames)
    gathered = lax.all_gather(embeddings, "band", axis=0, tiled=True)
    embed_width = embeddings.shape[1]
    partner_rows = gathered.reshape(-1, 128, embed_width)[partners]
    own_rows = embeddings.reshape(tile_count, 128, embed_width)
    inner_prod = jnp.einsum(
        "tkje,tie->tkji", partner_rows, own_rows, preferred_element_type=jnp.float32
    )
    affinity = (
        jnp.exp(0.5 * (inner_prod / math.sqrt(embed_width)))
        * (levels.astype(jnp.float32) / 8.0)[:, :, None, None]
        / 128.0
    )
    affinity = affinity.astype(jnp.bfloat16)
    far_degree = jnp.sum(affinity.astype(jnp.float32), axis=(1, 2)).reshape(frames)
    norm_scale = 1.0 / jnp.sqrt(near_degree + far_degree)

    def squares(residual):
        return total_over_devices(jnp.sum(residual * residual, axis=1))

    solution = jnp.zeros((channels, frames), jnp.float32)
    residual = labels
    direction = labels
    first_norm = jnp.sum(residual * residual, axis=1)
    for iteration in range(ITERS):
        lifted = (norm_scale[None, :] * direction).astype(jnp.bfloat16)
        padded = with_halo(lifted, ((("band", "seq"), 1),), RADIUS)
        windows = jnp.stack(
            [padded[:, position * 128 : position * 128 + window] for position in range(tile_count)],
            axis=0,
        )
        near_term = jnp.einsum(
            "tcw,twa->cta", windows, band_tiles, preferred_element_type=jnp.float32
        ).reshape(channels, frames)
        spread = jnp.transpose(band_gather(lifted), (1, 0, 2)).reshape(channels, -1, 128)
        far_tiles = spread[:, partners]
        far_term = jnp.einsum(
            "ctkj,tkji->cti", far_tiles, affinity, preferred_element_type=jnp.float32
        ).reshape(channels, frames)
        image = direction - spread_rate * norm_scale[None, :] * (near_term + far_term)
        sums = [jnp.sum(direction * image, axis=1)]
        last = iteration == ITERS - 1
        if not last:
            sums += [jnp.sum(residual * image, axis=1), jnp.sum(image * image, axis=1)]
        if iteration == 0:
            sums.append(first_norm)
        totals = total_over_devices(jnp.stack(sums))
        curve = totals[0]
        if iteration == 0:
            norm_now = totals[-1]
        alpha = norm_now / curve
        solution = solution + alpha[:, None] * direction
        if not last:
            residual = residual - alpha[:, None] * image
            norm_next = norm_now - 2.0 * alpha * totals[1] + alpha * alpha * totals[2]
            direction = residual + (norm_next / norm_now)[:, None] * direction
            norm_now = norm_next
    return solution


def solution(mesh):
    placed = (
        P(None, ("band", "seq")),
        P(("band", "seq")),
        P(("band", "seq"), None),
        P(),
        P(("band", "seq"), None),
        P(("band", "seq"), None),
        P(("band", "seq"), None),
    )
    return jax.shard_map(
        on_device, mesh=mesh, in_specs=placed, out_specs=P(None, ("band", "seq")), check_vma=False
    )
```

```python
import math

import jax
import jax.numpy as jnp
from jax import lax
from jax.sharding import PartitionSpec as P

RADIUS = 64
ITERS = 3


decay_len = 16.0
spread_rate = 0.9


def with_halo(cells, sides, width):
    for axis, dim in sides:
        count = lax.axis_size(axis)
        ends = count - 1
        head = lax.slice_in_dim(cells, 0, width, axis=dim)
        tail = lax.slice_in_dim(cells, cells.shape[dim] - width, cells.shape[dim], axis=dim)
        cells = jnp.concatenate(
            [
                lax.ppermute(tail, axis, [(i, (i + 1) % count) for i in range(ends)]),
                cells,
                lax.ppermute(head, axis, [((i + 1) % count, i) for i in range(ends)]),
            ],
            axis=dim,
        )
    return cells


def total_over_devices(values):
    for axis in ("seq", "band"):
        count = lax.axis_size(axis)
        spread = jnp.broadcast_to(values[None], (count,) + values.shape)
        rows = lax.all_to_all(spread, axis, split_axis=0, concat_axis=0, tiled=True)
        values = jnp.sum(rows, axis=0)
    return values


def band_gather(block):
    count = lax.axis_size("band")
    spread = jnp.broadcast_to(block[None], (count,) + block.shape)
    return lax.all_to_all(spread, "band", split_axis=0, concat_axis=0, tiled=True)


def on_device(posteriors, seed_mask, frame_perm, lengths, embeddings, partners, levels):
    channels, frames = posteriors.shape
    band_count = lax.axis_size("band")
    groups = lax.axis_size("seq")
    tile_count = frames // 128
    seeded = posteriors * seed_mask.astype(jnp.bfloat16)[None, :]
    ordered = jnp.take(seeded, frame_perm[0], axis=1).reshape(
        channels, band_count, frames // band_count
    )
    arrived = lax.all_to_all(ordered, "band", split_axis=1, concat_axis=1, tiled=True)
    labels = arrived.reshape(channels, frames).astype(jnp.float32)
    device = lax.axis_index("band") * groups + lax.axis_index("seq")
    frame_total = frames * band_count * groups
    window = 128 + 2 * RADIUS
    global_at = device * frames - RADIUS + jnp.arange(frames + 2 * RADIUS, dtype=jnp.int32)
    utt_ends = jnp.cumsum(lengths)
    owner_seg = jnp.sum((utt_ends[None, :] <= global_at[:, None]).astype(jnp.int32), axis=1)
    inside = (global_at >= 0) & (global_at < frame_total)
    tile_off = (jnp.arange(tile_count, dtype=jnp.int32) * 128)[:, None, None]
    win_pos = tile_off + jnp.arange(window, dtype=jnp.int32)[None, :, None]
    row_pos = tile_off + RADIUS + jnp.arange(128, dtype=jnp.int32)[None, None, :]
    offset = jnp.abs(win_pos - row_pos)
    linked = (
        (offset >= 1)
        & (offset <= RADIUS)
        & (owner_seg[win_pos] == owner_seg[row_pos])
        & inside[win_pos]
    )
    band_tiles = jnp.where(
        linked, jnp.exp(-offset.astype(jnp.float32) / decay_len), jnp.float32(0.0)
    ).astype(jnp.bfloat16)
    near_degree = jnp.sum(band_tiles.astype(jnp.float32), axis=1).reshape(frames)
    embed_width = embeddings.shape[1]
    split_rows = (tile_count - 1) * 128
    gathered = jnp.concatenate(
        [
            lax.all_gather(embeddings[:split_rows], "band", axis=0, tiled=False),
            band_gather(embeddings[split_rows:]),
        ],
        axis=1,
    )
    partner_rows = gathered.reshape(-1, 128, embed_width)[partners]
    own_rows = embeddings.reshape(tile_count, 128, embed_width)
    inner_prod = jnp.einsum(
        "tkje,tie->tkji", partner_rows, own_rows, preferred_element_type=jnp.float32
    )
    affinity = (
        jnp.exp(0.5 * (inner_prod / math.sqrt(embed_width)))
        * (levels.astype(jnp.float32) / 8.0)[:, :, None, None]
        / 128.0
    )
    affinity = affinity.astype(jnp.bfloat16)
    far_degree = jnp.sum(affinity.astype(jnp.float32), axis=(1, 2)).reshape(frames)
    norm_scale = 1.0 / jnp.sqrt(near_degree + far_degree)

    def squares(residual):
        return total_over_devices(jnp.sum(residual * residual, axis=1))

    solution = jnp.zeros((channels, frames), jnp.float32)
    residual = labels
    direction = labels
    first_norm = jnp.sum(residual * residual, axis=1)
    for iteration in range(ITERS):
        lifted = (norm_scale[None, :] * direction).astype(jnp.bfloat16)
        padded = with_halo(lifted, ((("band", "seq"), 1),), RADIUS)
        windows = jnp.stack(
            [padded[:, position * 128 : position * 128 + window] for position in range(tile_count)],
            axis=0,
        )
        near_term = jnp.einsum(
            "tcw,twa->cta", windows, band_tiles, preferred_element_type=jnp.float32
        ).reshape(channels, frames)
        spread = jnp.transpose(band_gather(lifted), (1, 0, 2)).reshape(channels, -1, 128)
        far_tiles = spread[:, partners]
        far_term = jnp.einsum(
            "ctkj,tkji->cti", far_tiles, affinity, preferred_element_type=jnp.float32
        ).reshape(channels, frames)
        image = direction - spread_rate * norm_scale[None, :] * (near_term + far_term)
        sums = [jnp.sum(direction * image, axis=1)]
        last = iteration == ITERS - 1
        if not last:
            sums += [jnp.sum(residual * image, axis=1), jnp.sum(image * image, axis=1)]
        if iteration == 0:
            sums.append(first_norm)
        totals = total_over_devices(jnp.stack(sums))
        curve = totals[0]
        if iteration == 0:
            norm_now = totals[-1]
        alpha = norm_now / curve
        solution = solution + alpha[:, None] * direction
        if not last:
            residual = residual - alpha[:, None] * image
            norm_next = norm_now - 2.0 * alpha * totals[1] + alpha * alpha * totals[2]
            direction = residual + (norm_next / norm_now)[:, None] * direction
            norm_now = norm_next
    return solution


def solution(mesh):
    placed = (
        P(None, ("band", "seq")),
        P(("band", "seq")),
        P(("band", "seq"), None),
        P(),
        P(("band", "seq"), None),
        P(("band", "seq"), None),
        P(("band", "seq"), None),
    )
    return jax.shard_map(
        on_device, mesh=mesh, in_specs=placed, out_specs=P(None, ("band", "seq")), check_vma=False
    )
```

```python
import math

import jax
import jax.numpy as jnp
from jax import lax
from jax.sharding import PartitionSpec as P

RADIUS = 64
ITERS = 3


decay_len = 16.0
spread_rate = 0.9


def with_halo(cells, sides, width):
    for axis, dim in sides:
        count = lax.axis_size(axis)
        ends = count - 1
        head = lax.slice_in_dim(cells, 0, width, axis=dim)
        tail = lax.slice_in_dim(cells, cells.shape[dim] - width, cells.shape[dim], axis=dim)
        cells = jnp.concatenate(
            [
                lax.ppermute(tail, axis, [(i, (i + 1) % count) for i in range(ends)]),
                cells,
                lax.ppermute(head, axis, [((i + 1) % count, i) for i in range(ends)]),
            ],
            axis=dim,
        )
    return cells


def total_over_devices(values):
    for axis in ("seq", "band"):
        count = lax.axis_size(axis)
        spread = jnp.broadcast_to(values[None], (count,) + values.shape)
        rows = lax.all_to_all(spread, axis, split_axis=0, concat_axis=0, tiled=True)
        values = jnp.sum(rows, axis=0)
    return values


def band_gather(block):
    count = lax.axis_size("band")
    spread = jnp.broadcast_to(block[None], (count,) + block.shape)
    return lax.all_to_all(spread, "band", split_axis=0, concat_axis=0, tiled=True)


def on_device(posteriors, seed_mask, frame_perm, lengths, embeddings, partners, levels):
    channels, frames = posteriors.shape
    band_count = lax.axis_size("band")
    groups = lax.axis_size("seq")
    tile_count = frames // 128
    seeded = posteriors * seed_mask.astype(jnp.bfloat16)[None, :]
    ordered = jnp.take(seeded, frame_perm[0], axis=1).reshape(
        channels, band_count, frames // band_count
    )
    arrived = lax.all_to_all(ordered, "band", split_axis=1, concat_axis=1, tiled=True)
    labels = arrived.reshape(channels, frames).astype(jnp.float32)
    device = lax.axis_index("band") * groups + lax.axis_index("seq")
    frame_total = frames * band_count * groups
    window = 128 + 2 * RADIUS
    global_at = device * frames - RADIUS + jnp.arange(frames + 2 * RADIUS, dtype=jnp.int32)
    utt_ends = jnp.cumsum(lengths)
    owner_seg = jnp.sum((utt_ends[None, :] <= global_at[:, None]).astype(jnp.int32), axis=1)
    inside = (global_at >= 0) & (global_at < frame_total)
    tile_off = (jnp.arange(tile_count, dtype=jnp.int32) * 128)[:, None, None]
    win_pos = tile_off + jnp.arange(window, dtype=jnp.int32)[None, :, None]
    row_pos = tile_off + RADIUS + jnp.arange(128, dtype=jnp.int32)[None, None, :]
    offset = jnp.abs(win_pos - row_pos)
    linked = (
        (offset >= 1)
        & (offset <= RADIUS)
        & (owner_seg[win_pos] == owner_seg[row_pos])
        & inside[win_pos]
    )
    band_tiles = jnp.where(
        linked, jnp.exp(-offset.astype(jnp.float32) / decay_len), jnp.float32(0.0)
    ).astype(jnp.bfloat16)
    near_degree = jnp.sum(band_tiles.astype(jnp.float32), axis=1).reshape(frames)
    gathered = lax.all_gather(embeddings, "band", axis=0, tiled=True)
    labels_band = band_gather(arrived.reshape(channels, frames))
    labels_band, gathered = lax.optimization_barrier((labels_band, gathered))
    embed_width = embeddings.shape[1]
    partner_rows = gathered.reshape(-1, 128, embed_width)[partners]
    own_rows = embeddings.reshape(tile_count, 128, embed_width)
    inner_prod = jnp.einsum(
        "tkje,tie->tkji", partner_rows, own_rows, preferred_element_type=jnp.float32
    )
    affinity = (
        jnp.exp(0.5 * (inner_prod / math.sqrt(embed_width)))
        * (levels.astype(jnp.float32) / 8.0)[:, :, None, None]
        / 128.0
    )
    affinity = affinity.astype(jnp.bfloat16)
    far_degree = jnp.sum(affinity.astype(jnp.float32), axis=(1, 2)).reshape(frames)
    norm_scale = 1.0 / jnp.sqrt(near_degree + far_degree)

    def squares(residual):
        return total_over_devices(jnp.sum(residual * residual, axis=1))

    solution = jnp.zeros((channels, frames), jnp.float32)
    residual = labels
    direction = labels
    first_norm = jnp.sum(residual * residual, axis=1)
    scale_band = band_gather(norm_scale)
    for iteration in range(ITERS):
        lifted = (norm_scale[None, :] * direction).astype(jnp.bfloat16)
        padded = with_halo(lifted, ((("band", "seq"), 1),), RADIUS)
        windows = jnp.stack(
            [padded[:, position * 128 : position * 128 + window] for position in range(tile_count)],
            axis=0,
        )
        near_term = jnp.einsum(
            "tcw,twa->cta", windows, band_tiles, preferred_element_type=jnp.float32
        ).reshape(channels, frames)
        if iteration == 0:
            lifted_band = (scale_band[:, None, :] * labels_band.astype(jnp.float32)).astype(jnp.bfloat16)
        else:
            lifted_band = band_gather(lifted)
        spread = jnp.transpose(lifted_band, (1, 0, 2)).reshape(channels, -1, 128)
        far_tiles = spread[:, partners]
        far_term = jnp.einsum(
            "ctkj,tkji->cti", far_tiles, affinity, preferred_element_type=jnp.float32
        ).reshape(channels, frames)
        image = direction - spread_rate * norm_scale[None, :] * (near_term + far_term)
        sums = [jnp.sum(direction * image, axis=1)]
        last = iteration == ITERS - 1
        if not last:
            sums += [jnp.sum(residual * image, axis=1), jnp.sum(image * image, axis=1)]
        if iteration == 0:
            sums.append(first_norm)
        totals = total_over_devices(jnp.stack(sums))
        curve = totals[0]
        if iteration == 0:
            norm_now = totals[-1]
        alpha = norm_now / curve
        solution = solution + alpha[:, None] * direction
        if not last:
            residual = residual - alpha[:, None] * image
            norm_next = norm_now - 2.0 * alpha * totals[1] + alpha * alpha * totals[2]
            direction = residual + (norm_next / norm_now)[:, None] * direction
            norm_now = norm_next
    return solution


def solution(mesh):
    placed = (
        P(None, ("band", "seq")),
        P(("band", "seq")),
        P(("band", "seq"), None),
        P(),
        P(("band", "seq"), None),
        P(("band", "seq"), None),
        P(("band", "seq"), None),
    )
    return jax.shard_map(
        on_device, mesh=mesh, in_specs=placed, out_specs=P(None, ("band", "seq")), check_vma=False
    )
```

```python
import math

import jax
import jax.numpy as jnp
from jax import lax
from jax.sharding import PartitionSpec as P

RADIUS = 64
ITERS = 3


decay_len = 16.0
spread_rate = 0.9


def with_halo(cells, sides, width):
    for axis, dim in sides:
        count = lax.axis_size(axis)
        ends = count - 1
        head = lax.slice_in_dim(cells, 0, width, axis=dim)
        tail = lax.slice_in_dim(cells, cells.shape[dim] - width, cells.shape[dim], axis=dim)
        cells = jnp.concatenate(
            [
                lax.ppermute(tail, axis, [(i, (i + 1) % count) for i in range(ends)]),
                cells,
                lax.ppermute(head, axis, [((i + 1) % count, i) for i in range(ends)]),
            ],
            axis=dim,
        )
    return cells


def total_over_devices(values):
    values = lax.optimization_barrier(lax.psum(values, "seq"))
    return lax.psum(values, "band")


def band_gather(block):
    count = lax.axis_size("band")
    spread = jnp.broadcast_to(block[None], (count,) + block.shape)
    return lax.all_to_all(spread, "band", split_axis=0, concat_axis=0, tiled=True)


def on_device(posteriors, seed_mask, frame_perm, lengths, embeddings, partners, levels):
    channels, frames = posteriors.shape
    band_count = lax.axis_size("band")
    groups = lax.axis_size("seq")
    tile_count = frames // 128
    seeded = posteriors * seed_mask.astype(jnp.bfloat16)[None, :]
    ordered = jnp.take(seeded, frame_perm[0], axis=1).reshape(
        channels, band_count, frames // band_count
    )
    arrived = lax.all_to_all(ordered, "band", split_axis=1, concat_axis=1, tiled=True)
    labels = arrived.reshape(channels, frames).astype(jnp.float32)
    device = lax.axis_index("band") * groups + lax.axis_index("seq")
    frame_total = frames * band_count * groups
    window = 128 + 2 * RADIUS
    global_at = device * frames - RADIUS + jnp.arange(frames + 2 * RADIUS, dtype=jnp.int32)
    utt_ends = jnp.cumsum(lengths)
    owner_seg = jnp.sum((utt_ends[None, :] <= global_at[:, None]).astype(jnp.int32), axis=1)
    inside = (global_at >= 0) & (global_at < frame_total)
    tile_off = (jnp.arange(tile_count, dtype=jnp.int32) * 128)[:, None, None]
    win_pos = tile_off + jnp.arange(window, dtype=jnp.int32)[None, :, None]
    row_pos = tile_off + RADIUS + jnp.arange(128, dtype=jnp.int32)[None, None, :]
    offset = jnp.abs(win_pos - row_pos)
    linked = (
        (offset >= 1)
        & (offset <= RADIUS)
        & (owner_seg[win_pos] == owner_seg[row_pos])
        & inside[win_pos]
    )
    band_tiles = jnp.where(
        linked, jnp.exp(-offset.astype(jnp.float32) / decay_len), jnp.float32(0.0)
    ).astype(jnp.bfloat16)
    near_degree = jnp.sum(band_tiles.astype(jnp.float32), axis=1).reshape(frames)
    gathered = lax.all_gather(embeddings, "band", axis=0, tiled=True)
    labels_band = band_gather(arrived.reshape(channels, frames))
    labels_band, gathered = lax.optimization_barrier((labels_band, gathered))
    embed_width = embeddings.shape[1]
    partner_rows = gathered.reshape(-1, 128, embed_width)[partners]
    own_rows = embeddings.reshape(tile_count, 128, embed_width)
    inner_prod = jnp.einsum(
        "tkje,tie->tkji", partner_rows, own_rows, preferred_element_type=jnp.float32
    )
    affinity = (
        jnp.exp(0.5 * (inner_prod / math.sqrt(embed_width)))
        * (levels.astype(jnp.float32) / 8.0)[:, :, None, None]
        / 128.0
    )
    affinity = affinity.astype(jnp.bfloat16)
    far_degree = jnp.sum(affinity.astype(jnp.float32), axis=(1, 2)).reshape(frames)
    norm_scale = 1.0 / jnp.sqrt(near_degree + far_degree)

    def squares(residual):
        return total_over_devices(jnp.sum(residual * residual, axis=1))

    solution = jnp.zeros((channels, frames), jnp.float32)
    residual = labels
    direction = labels
    first_norm = jnp.sum(residual * residual, axis=1)
    scale_band = band_gather(norm_scale)
    for iteration in range(ITERS):
        lifted = (norm_scale[None, :] * direction).astype(jnp.bfloat16)
        padded = with_halo(lifted, ((("band", "seq"), 1),), RADIUS)
        windows = jnp.stack(
            [padded[:, position * 128 : position * 128 + window] for position in range(tile_count)],
            axis=0,
        )
        near_term = jnp.einsum(
            "tcw,twa->cta", windows, band_tiles, preferred_element_type=jnp.float32
        ).reshape(channels, frames)
        if iteration == 0:
            lifted_band = (scale_band[:, None, :] * labels_band.astype(jnp.float32)).astype(jnp.bfloat16)
        else:
            lifted_band = band_gather(lifted)
        spread = jnp.transpose(lifted_band, (1, 0, 2)).reshape(channels, -1, 128)
        far_tiles = spread[:, partners]
        far_term = jnp.einsum(
            "ctkj,tkji->cti", far_tiles, affinity, preferred_element_type=jnp.float32
        ).reshape(channels, frames)
        image = direction - spread_rate * norm_scale[None, :] * (near_term + far_term)
        sums = [jnp.sum(direction * image, axis=1)]
        last = iteration == ITERS - 1
        if not last:
            sums += [jnp.sum(residual * image, axis=1), jnp.sum(image * image, axis=1)]
        if iteration == 0:
            sums.append(first_norm)
        totals = total_over_devices(jnp.stack(sums))
        curve = totals[0]
        if iteration == 0:
            norm_now = totals[-1]
        alpha = norm_now / curve
        solution = solution + alpha[:, None] * direction
        if not last:
            residual = residual - alpha[:, None] * image
            norm_next = norm_now - 2.0 * alpha * totals[1] + alpha * alpha * totals[2]
            direction = residual + (norm_next / norm_now)[:, None] * direction
            norm_now = norm_next
    return solution


def solution(mesh):
    placed = (
        P(None, ("band", "seq")),
        P(("band", "seq")),
        P(("band", "seq"), None),
        P(),
        P(("band", "seq"), None),
        P(("band", "seq"), None),
        P(("band", "seq"), None),
    )
    return jax.shard_map(
        on_device, mesh=mesh, in_specs=placed, out_specs=P(None, ("band", "seq")), check_vma=False
    )
```

```python
import math

import jax
import jax.numpy as jnp
from jax import lax
from jax.experimental import pallas as pl
from jax.experimental.pallas import tpu as pltpu
from jax.sharding import PartitionSpec as P

RADIUS = 64
ITERS = 3


decay_len = 16.0
spread_rate = 0.9


def with_halo(cells, sides, width):
    for axis, dim in sides:
        count = lax.axis_size(axis)
        ends = count - 1
        head = lax.slice_in_dim(cells, 0, width, axis=dim)
        tail = lax.slice_in_dim(cells, cells.shape[dim] - width, cells.shape[dim], axis=dim)
        cells = jnp.concatenate(
            [
                lax.ppermute(tail, axis, [(i, (i + 1) % count) for i in range(ends)]),
                cells,
                lax.ppermute(head, axis, [((i + 1) % count, i) for i in range(ends)]),
            ],
            axis=dim,
        )
    return cells


def total_over_devices(values):
    for axis in ("seq", "band"):
        count = lax.axis_size(axis)
        spread = jnp.broadcast_to(values[None], (count,) + values.shape)
        rows = lax.all_to_all(spread, axis, split_axis=0, concat_axis=0, tiled=True)
        values = jnp.sum(rows, axis=0)
    return values


def band_gather(block):
    count = lax.axis_size("band")
    spread = jnp.broadcast_to(block[None], (count,) + block.shape)
    return lax.all_to_all(spread, "band", split_axis=0, concat_axis=0, tiled=True)


SLOT_BLOCK = 8


def affinity_kernel(part_ref, lev_ref, own_ref, *refs):
    partner_refs = refs[:SLOT_BLOCK]
    aff_ref, deg_ref = refs[SLOT_BLOCK], refs[SLOT_BLOCK + 1]
    tile = pl.program_id(0)
    block = pl.program_id(1)
    own = own_ref[0]
    total = jnp.zeros((1, own.shape[0]), jnp.float32)
    for slot in range(SLOT_BLOCK):
        rows = partner_refs[slot][0]
        inner = lax.dot_general(
            rows, own, (((1,), (1,)), ((), ())), preferred_element_type=jnp.float32
        )
        level = lev_ref[tile, block * SLOT_BLOCK + slot].astype(jnp.float32)
        weight = (
            jnp.exp(0.5 * (inner / math.sqrt(own.shape[1]))) * (level / 8.0) / 128.0
        ).astype(jnp.bfloat16)
        aff_ref[0, slot] = weight
        total = total + jnp.sum(weight.astype(jnp.float32), axis=0, keepdims=True)
    deg_ref[0, 0] = total


def affinity_blocks(own_rows, group_rows, partners, levels):
    tiles, width, embed = own_rows.shape
    slots = partners.shape[1]
    blocks = slots // SLOT_BLOCK

    def partner_spec(slot):
        return pl.BlockSpec(
            (1, width, embed), lambda t, b, part, lev: (part[t, b * SLOT_BLOCK + slot], 0, 0)
        )

    grid_spec = pltpu.PrefetchScalarGridSpec(
        num_scalar_prefetch=2,
        grid=(tiles, blocks),
        in_specs=[pl.BlockSpec((1, width, embed), lambda t, b, part, lev: (t, 0, 0))]
        + [partner_spec(slot) for slot in range(SLOT_BLOCK)],
        out_specs=[
            pl.BlockSpec((1, SLOT_BLOCK, width, width), lambda t, b, part, lev: (t, b, 0, 0)),
            pl.BlockSpec((1, 1, 1, width), lambda t, b, part, lev: (t, b, 0, 0)),
        ],
    )
    affinity, degree = pl.pallas_call(
        affinity_kernel,
        grid_spec=grid_spec,
        out_shape=[
            jax.ShapeDtypeStruct((tiles, slots, width, width), jnp.bfloat16),
            jax.ShapeDtypeStruct((tiles, blocks, 1, width), jnp.float32),
        ],
    )(partners, levels, own_rows, *([group_rows] * SLOT_BLOCK))
    return affinity, jnp.sum(degree[:, :, 0, :], axis=1).reshape(-1)


def on_device(posteriors, seed_mask, frame_perm, lengths, embeddings, partners, levels):
    channels, frames = posteriors.shape
    band_count = lax.axis_size("band")
    groups = lax.axis_size("seq")
    tile_count = frames // 128
    seeded = posteriors * seed_mask.astype(jnp.bfloat16)[None, :]
    ordered = jnp.take(seeded, frame_perm[0], axis=1).reshape(
        channels, band_count, frames // band_count
    )
    arrived = lax.all_to_all(ordered, "band", split_axis=1, concat_axis=1, tiled=True)
    labels = arrived.reshape(channels, frames).astype(jnp.float32)
    device = lax.axis_index("band") * groups + lax.axis_index("seq")
    frame_total = frames * band_count * groups
    window = 128 + 2 * RADIUS
    global_at = device * frames - RADIUS + jnp.arange(frames + 2 * RADIUS, dtype=jnp.int32)
    utt_ends = jnp.cumsum(lengths)
    owner_seg = jnp.sum((utt_ends[None, :] <= global_at[:, None]).astype(jnp.int32), axis=1)
    inside = (global_at >= 0) & (global_at < frame_total)
    tile_off = (jnp.arange(tile_count, dtype=jnp.int32) * 128)[:, None, None]
    win_pos = tile_off + jnp.arange(window, dtype=jnp.int32)[None, :, None]
    row_pos = tile_off + RADIUS + jnp.arange(128, dtype=jnp.int32)[None, None, :]
    offset = jnp.abs(win_pos - row_pos)
    linked = (
        (offset >= 1)
        & (offset <= RADIUS)
        & (owner_seg[win_pos] == owner_seg[row_pos])
        & inside[win_pos]
    )
    band_tiles = jnp.where(
        linked, jnp.exp(-offset.astype(jnp.float32) / decay_len), jnp.float32(0.0)
    ).astype(jnp.bfloat16)
    near_degree = jnp.sum(band_tiles.astype(jnp.float32), axis=1).reshape(frames)
    gathered = lax.all_gather(embeddings, "band", axis=0, tiled=True)
    labels_band = band_gather(arrived.reshape(channels, frames))
    labels_band, gathered = lax.optimization_barrier((labels_band, gathered))
    embed_width = embeddings.shape[1]
    own_rows = embeddings.reshape(tile_count, 128, embed_width)
    affinity, far_degree = affinity_blocks(
        own_rows, gathered.reshape(-1, 128, embed_width), partners, levels
    )
    norm_scale = 1.0 / jnp.sqrt(near_degree + far_degree)

    def squares(residual):
        return total_over_devices(jnp.sum(residual * residual, axis=1))

    solution = jnp.zeros((channels, frames), jnp.float32)
    residual = labels
    direction = labels
    first_norm = jnp.sum(residual * residual, axis=1)
    scale_band = band_gather(norm_scale)
    for iteration in range(ITERS):
        lifted = (norm_scale[None, :] * direction).astype(jnp.bfloat16)
        padded = with_halo(lifted, ((("band", "seq"), 1),), RADIUS)
        windows = jnp.stack(
            [padded[:, position * 128 : position * 128 + window] for position in range(tile_count)],
            axis=0,
        )
        near_term = jnp.einsum(
            "tcw,twa->cta", windows, band_tiles, preferred_element_type=jnp.float32
        ).reshape(channels, frames)
        if iteration == 0:
            lifted_band = (scale_band[:, None, :] * labels_band.astype(jnp.float32)).astype(jnp.bfloat16)
        else:
            lifted_band = band_gather(lifted)
        spread = jnp.transpose(lifted_band, (1, 0, 2)).reshape(channels, -1, 128)
        far_tiles = spread[:, partners]
        far_term = jnp.einsum(
            "ctkj,tkji->cti", far_tiles, affinity, preferred_element_type=jnp.float32
        ).reshape(channels, frames)
        image = direction - spread_rate * norm_scale[None, :] * (near_term + far_term)
        sums = [jnp.sum(direction * image, axis=1)]
        last = iteration == ITERS - 1
        if not last:
            sums += [jnp.sum(residual * image, axis=1), jnp.sum(image * image, axis=1)]
        if iteration == 0:
            sums.append(first_norm)
        totals = total_over_devices(jnp.stack(sums))
        curve = totals[0]
        if iteration == 0:
            norm_now = totals[-1]
        alpha = norm_now / curve
        solution = solution + alpha[:, None] * direction
        if not last:
            residual = residual - alpha[:, None] * image
            norm_next = norm_now - 2.0 * alpha * totals[1] + alpha * alpha * totals[2]
            direction = residual + (norm_next / norm_now)[:, None] * direction
            norm_now = norm_next
    return solution


def solution(mesh):
    placed = (
        P(None, ("band", "seq")),
        P(("band", "seq")),
        P(("band", "seq"), None),
        P(),
        P(("band", "seq"), None),
        P(("band", "seq"), None),
        P(("band", "seq"), None),
    )
    return jax.shard_map(
        on_device, mesh=mesh, in_specs=placed, out_specs=P(None, ("band", "seq")), check_vma=False
    )
```

```python
import math

import jax
import jax.numpy as jnp
from jax import lax
from jax.sharding import PartitionSpec as P

RADIUS = 64
ITERS = 3


decay_len = 16.0
spread_rate = 0.9


def with_halo(cells, sides, width):
    for axis, dim in sides:
        count = lax.axis_size(axis)
        ends = count - 1
        head = lax.slice_in_dim(cells, 0, width, axis=dim)
        tail = lax.slice_in_dim(cells, cells.shape[dim] - width, cells.shape[dim], axis=dim)
        cells = jnp.concatenate(
            [
                lax.ppermute(tail, axis, [(i, (i + 1) % count) for i in range(ends)]),
                cells,
                lax.ppermute(head, axis, [((i + 1) % count, i) for i in range(ends)]),
            ],
            axis=dim,
        )
    return cells


def total_over_devices(values):
    for axis in ("seq", "band"):
        count = lax.axis_size(axis)
        spread = jnp.broadcast_to(values[None], (count,) + values.shape)
        rows = lax.all_to_all(spread, axis, split_axis=0, concat_axis=0, tiled=True)
        values = jnp.sum(rows, axis=0)
    return values


def band_gather(block):
    count = lax.axis_size("band")
    spread = jnp.broadcast_to(block[None], (count,) + block.shape)
    return lax.all_to_all(spread, "band", split_axis=0, concat_axis=0, tiled=True)


def on_device(posteriors, seed_mask, frame_perm, lengths, embeddings, partners, levels):
    channels, frames = posteriors.shape
    band_count = lax.axis_size("band")
    groups = lax.axis_size("seq")
    tile_count = frames // 128
    seeded = posteriors * seed_mask.astype(jnp.bfloat16)[None, :]
    ordered = jnp.take(seeded, frame_perm[0], axis=1).reshape(
        channels, band_count, frames // band_count
    )
    from_bands = band_gather(ordered)
    labels_band = jnp.transpose(from_bands, (2, 1, 0, 3)).reshape(band_count, channels, frames)
    arrived = lax.dynamic_index_in_dim(labels_band, lax.axis_index("band"), axis=0, keepdims=False)
    labels = arrived.astype(jnp.float32)
    device = lax.axis_index("band") * groups + lax.axis_index("seq")
    frame_total = frames * band_count * groups
    window = 128 + 2 * RADIUS
    global_at = device * frames - RADIUS + jnp.arange(frames + 2 * RADIUS, dtype=jnp.int32)
    utt_ends = jnp.cumsum(lengths)
    owner_seg = jnp.sum((utt_ends[None, :] <= global_at[:, None]).astype(jnp.int32), axis=1)
    inside = (global_at >= 0) & (global_at < frame_total)
    tile_off = (jnp.arange(tile_count, dtype=jnp.int32) * 128)[:, None, None]
    win_pos = tile_off + jnp.arange(window, dtype=jnp.int32)[None, :, None]
    row_pos = tile_off + RADIUS + jnp.arange(128, dtype=jnp.int32)[None, None, :]
    offset = jnp.abs(win_pos - row_pos)
    linked = (
        (offset >= 1)
        & (offset <= RADIUS)
        & (owner_seg[win_pos] == owner_seg[row_pos])
        & inside[win_pos]
    )
    band_tiles = jnp.where(
        linked, jnp.exp(-offset.astype(jnp.float32) / decay_len), jnp.float32(0.0)
    ).astype(jnp.bfloat16)
    near_degree = jnp.sum(band_tiles.astype(jnp.float32), axis=1).reshape(frames)
    gathered = lax.all_gather(embeddings, "band", axis=0, tiled=True)
    labels_band, gathered = lax.optimization_barrier((labels_band, gathered))
    embed_width = embeddings.shape[1]
    partner_rows = gathered.reshape(-1, 128, embed_width)[partners]
    own_rows = embeddings.reshape(tile_count, 128, embed_width)
    inner_prod = jnp.einsum(
        "tkje,tie->tkji", partner_rows, own_rows, preferred_element_type=jnp.float32
    )
    affinity = (
        jnp.exp(0.5 * (inner_prod / math.sqrt(embed_width)))
        * (levels.astype(jnp.float32) / 8.0)[:, :, None, None]
        / 128.0
    )
    affinity = affinity.astype(jnp.bfloat16)
    far_degree = jnp.sum(affinity.astype(jnp.float32), axis=(1, 2)).reshape(frames)
    norm_scale = 1.0 / jnp.sqrt(near_degree + far_degree)

    def squares(residual):
        return total_over_devices(jnp.sum(residual * residual, axis=1))

    solution = jnp.zeros((channels, frames), jnp.float32)
    residual = labels
    direction = labels
    first_norm = jnp.sum(residual * residual, axis=1)
    scale_band = band_gather(norm_scale)
    for iteration in range(ITERS):
        lifted = (norm_scale[None, :] * direction).astype(jnp.bfloat16)
        padded = with_halo(lifted, ((("band", "seq"), 1),), RADIUS)
        windows = jnp.stack(
            [padded[:, position * 128 : position * 128 + window] for position in range(tile_count)],
            axis=0,
        )
        near_term = jnp.einsum(
            "tcw,twa->cta", windows, band_tiles, preferred_element_type=jnp.float32
        ).reshape(channels, frames)
        if iteration == 0:
            lifted_band = (scale_band[:, None, :] * labels_band.astype(jnp.float32)).astype(jnp.bfloat16)
        else:
            lifted_band = band_gather(lifted)
        spread = jnp.transpose(lifted_band, (1, 0, 2)).reshape(channels, -1, 128)
        far_tiles = spread[:, partners]
        far_term = jnp.einsum(
            "ctkj,tkji->cti", far_tiles, affinity, preferred_element_type=jnp.float32
        ).reshape(channels, frames)
        image = direction - spread_rate * norm_scale[None, :] * (near_term + far_term)
        sums = [jnp.sum(direction * image, axis=1)]
        last = iteration == ITERS - 1
        if not last:
            sums += [jnp.sum(residual * image, axis=1), jnp.sum(image * image, axis=1)]
        if iteration == 0:
            sums.append(first_norm)
        totals = total_over_devices(jnp.stack(sums))
        curve = totals[0]
        if iteration == 0:
            norm_now = totals[-1]
        alpha = norm_now / curve
        solution = solution + alpha[:, None] * direction
        if not last:
            residual = residual - alpha[:, None] * image
            norm_next = norm_now - 2.0 * alpha * totals[1] + alpha * alpha * totals[2]
            direction = residual + (norm_next / norm_now)[:, None] * direction
            norm_now = norm_next
    return solution


def solution(mesh):
    placed = (
        P(None, ("band", "seq")),
        P(("band", "seq")),
        P(("band", "seq"), None),
        P(),
        P(("band", "seq"), None),
        P(("band", "seq"), None),
        P(("band", "seq"), None),
    )
    return jax.shard_map(
        on_device, mesh=mesh, in_specs=placed, out_specs=P(None, ("band", "seq")), check_vma=False
    )
```

```python
import math

import jax
import jax.numpy as jnp
from jax import lax
from jax.sharding import PartitionSpec as P

RADIUS = 64
ITERS = 3


decay_len = 16.0
spread_rate = 0.9


def with_halo(cells, sides, width):
    for axis, dim in sides:
        count = lax.axis_size(axis)
        ends = count - 1
        head = lax.slice_in_dim(cells, 0, width, axis=dim)
        tail = lax.slice_in_dim(cells, cells.shape[dim] - width, cells.shape[dim], axis=dim)
        cells = jnp.concatenate(
            [
                lax.ppermute(tail, axis, [(i, (i + 1) % count) for i in range(ends)]),
                cells,
                lax.ppermute(head, axis, [((i + 1) % count, i) for i in range(ends)]),
            ],
            axis=dim,
        )
    return cells


def total_over_devices(values):
    for axis in ("band", "seq"):
        count = lax.axis_size(axis)
        spread = jnp.broadcast_to(values[None], (count,) + values.shape)
        rows = lax.all_to_all(spread, axis, split_axis=0, concat_axis=0, tiled=True)
        values = jnp.sum(rows, axis=0)
    return values


def band_gather(block):
    count = lax.axis_size("band")
    spread = jnp.broadcast_to(block[None], (count,) + block.shape)
    return lax.all_to_all(spread, "band", split_axis=0, concat_axis=0, tiled=True)


def on_device(posteriors, seed_mask, frame_perm, lengths, embeddings, partners, levels):
    channels, frames = posteriors.shape
    band_count = lax.axis_size("band")
    groups = lax.axis_size("seq")
    tile_count = frames // 128
    seeded = posteriors * seed_mask.astype(jnp.bfloat16)[None, :]
    ordered = jnp.take(seeded, frame_perm[0], axis=1).reshape(
        channels, band_count, frames // band_count
    )
    arrived = lax.all_to_all(ordered, "band", split_axis=1, concat_axis=1, tiled=True)
    labels = arrived.reshape(channels, frames).astype(jnp.float32)
    device = lax.axis_index("band") * groups + lax.axis_index("seq")
    frame_total = frames * band_count * groups
    window = 128 + 2 * RADIUS
    global_at = device * frames - RADIUS + jnp.arange(frames + 2 * RADIUS, dtype=jnp.int32)
    utt_ends = jnp.cumsum(lengths)
    owner_seg = jnp.sum((utt_ends[None, :] <= global_at[:, None]).astype(jnp.int32), axis=1)
    inside = (global_at >= 0) & (global_at < frame_total)
    tile_off = (jnp.arange(tile_count, dtype=jnp.int32) * 128)[:, None, None]
    win_pos = tile_off + jnp.arange(window, dtype=jnp.int32)[None, :, None]
    row_pos = tile_off + RADIUS + jnp.arange(128, dtype=jnp.int32)[None, None, :]
    offset = jnp.abs(win_pos - row_pos)
    linked = (
        (offset >= 1)
        & (offset <= RADIUS)
        & (owner_seg[win_pos] == owner_seg[row_pos])
        & inside[win_pos]
    )
    band_tiles = jnp.where(
        linked, jnp.exp(-offset.astype(jnp.float32) / decay_len), jnp.float32(0.0)
    ).astype(jnp.bfloat16)
    near_degree = jnp.sum(band_tiles.astype(jnp.float32), axis=1).reshape(frames)
    gathered = lax.all_gather(embeddings, "band", axis=0, tiled=True)
    labels_band = band_gather(arrived.reshape(channels, frames))
    labels_band, gathered = lax.optimization_barrier((labels_band, gathered))
    embed_width = embeddings.shape[1]
    partner_rows = gathered.reshape(-1, 128, embed_width)[partners]
    own_rows = embeddings.reshape(tile_count, 128, embed_width)
    inner_prod = jnp.einsum(
        "tkje,tie->tkji", partner_rows, own_rows, preferred_element_type=jnp.float32
    )
    affinity = (
        jnp.exp(0.5 * (inner_prod / math.sqrt(embed_width)))
        * (levels.astype(jnp.float32) / 8.0)[:, :, None, None]
        / 128.0
    )
    affinity = affinity.astype(jnp.bfloat16)
    far_degree = jnp.sum(affinity.astype(jnp.float32), axis=(1, 2)).reshape(frames)
    norm_scale = 1.0 / jnp.sqrt(near_degree + far_degree)

    def squares(residual):
        return total_over_devices(jnp.sum(residual * residual, axis=1))

    solution = jnp.zeros((channels, frames), jnp.float32)
    residual = labels
    direction = labels
    first_norm = jnp.sum(residual * residual, axis=1)
    scale_band = band_gather(norm_scale)
    for iteration in range(ITERS):
        lifted = (norm_scale[None, :] * direction).astype(jnp.bfloat16)
        padded = with_halo(lifted, ((("band", "seq"), 1),), RADIUS)
        windows = jnp.stack(
            [padded[:, position * 128 : position * 128 + window] for position in range(tile_count)],
            axis=0,
        )
        near_term = jnp.einsum(
            "tcw,twa->cta", windows, band_tiles, preferred_element_type=jnp.float32
        ).reshape(channels, frames)
        if iteration == 0:
            lifted_band = (scale_band[:, None, :] * labels_band.astype(jnp.float32)).astype(jnp.bfloat16)
        else:
            lifted_band = band_gather(lifted)
        spread = jnp.transpose(lifted_band, (1, 0, 2)).reshape(channels, -1, 128)
        far_tiles = spread[:, partners]
        far_term = jnp.einsum(
            "ctkj,tkji->cti", far_tiles, affinity, preferred_element_type=jnp.float32
        ).reshape(channels, frames)
        image = direction - spread_rate * norm_scale[None, :] * (near_term + far_term)
        sums = [jnp.sum(direction * image, axis=1)]
        last = iteration == ITERS - 1
        if not last:
            sums += [jnp.sum(residual * image, axis=1), jnp.sum(image * image, axis=1)]
        if iteration == 0:
            sums.append(first_norm)
        totals = total_over_devices(jnp.stack(sums))
        curve = totals[0]
        if iteration == 0:
            norm_now = totals[-1]
        alpha = norm_now / curve
        solution = solution + alpha[:, None] * direction
        if not last:
            residual = residual - alpha[:, None] * image
            norm_next = norm_now - 2.0 * alpha * totals[1] + alpha * alpha * totals[2]
            direction = residual + (norm_next / norm_now)[:, None] * direction
            norm_now = norm_next
    return solution


def solution(mesh):
    placed = (
        P(None, ("band", "seq")),
        P(("band", "seq")),
        P(("band", "seq"), None),
        P(),
        P(("band", "seq"), None),
        P(("band", "seq"), None),
        P(("band", "seq"), None),
    )
    return jax.shard_map(
        on_device, mesh=mesh, in_specs=placed, out_specs=P(None, ("band", "seq")), check_vma=False
    )
```

```python
import math

import jax
import jax.numpy as jnp
from jax import lax
from jax.sharding import PartitionSpec as P

RADIUS = 64
ITERS = 3


decay_len = 16.0
spread_rate = 0.9


def with_halo(cells, sides, width):
    for axis, dim in sides:
        count = lax.axis_size(axis)
        ends = count - 1
        head = lax.slice_in_dim(cells, 0, width, axis=dim)
        tail = lax.slice_in_dim(cells, cells.shape[dim] - width, cells.shape[dim], axis=dim)
        cells = jnp.concatenate(
            [
                lax.ppermute(tail, axis, [(i, (i + 1) % count) for i in range(ends)]),
                cells,
                lax.ppermute(head, axis, [((i + 1) % count, i) for i in range(ends)]),
            ],
            axis=dim,
        )
    return cells


def total_over_devices(values):
    for axis in ("seq", "band"):
        count = lax.axis_size(axis)
        spread = jnp.broadcast_to(values[None], (count,) + values.shape)
        rows = lax.all_to_all(spread, axis, split_axis=0, concat_axis=0, tiled=True)
        values = jnp.sum(rows, axis=0)
    return values


def band_gather(block):
    count = lax.axis_size("band")
    spread = jnp.broadcast_to(block[None], (count,) + block.shape)
    return lax.all_to_all(spread, "band", split_axis=0, concat_axis=0, tiled=True)


def on_device(posteriors, seed_mask, frame_perm, lengths, embeddings, partners, levels):
    channels, frames = posteriors.shape
    band_count = lax.axis_size("band")
    groups = lax.axis_size("seq")
    tile_count = frames // 128
    seeded = posteriors * seed_mask.astype(jnp.bfloat16)[None, :]
    ordered = jnp.take(seeded, frame_perm[0], axis=1).reshape(
        channels, band_count, frames // band_count
    )
    embed_width = embeddings.shape[1]
    carried = jnp.concatenate([embeddings, ordered.reshape(channels, frames).T], axis=1)
    carried = lax.all_gather(carried, "band", axis=0, tiled=True)
    gathered = carried[:, :embed_width]
    labels_band = jnp.transpose(
        carried[:, embed_width:].reshape(band_count, band_count, frames // band_count, channels),
        (1, 3, 0, 2),
    ).reshape(band_count, channels, frames)
    arrived = lax.dynamic_index_in_dim(labels_band, lax.axis_index("band"), axis=0, keepdims=False)
    labels = arrived.astype(jnp.float32)
    device = lax.axis_index("band") * groups + lax.axis_index("seq")
    frame_total = frames * band_count * groups
    window = 128 + 2 * RADIUS
    global_at = device * frames - RADIUS + jnp.arange(frames + 2 * RADIUS, dtype=jnp.int32)
    utt_ends = jnp.cumsum(lengths)
    owner_seg = jnp.sum((utt_ends[None, :] <= global_at[:, None]).astype(jnp.int32), axis=1)
    inside = (global_at >= 0) & (global_at < frame_total)
    tile_off = (jnp.arange(tile_count, dtype=jnp.int32) * 128)[:, None, None]
    win_pos = tile_off + jnp.arange(window, dtype=jnp.int32)[None, :, None]
    row_pos = tile_off + RADIUS + jnp.arange(128, dtype=jnp.int32)[None, None, :]
    offset = jnp.abs(win_pos - row_pos)
    linked = (
        (offset >= 1)
        & (offset <= RADIUS)
        & (owner_seg[win_pos] == owner_seg[row_pos])
        & inside[win_pos]
    )
    band_tiles = jnp.where(
        linked, jnp.exp(-offset.astype(jnp.float32) / decay_len), jnp.float32(0.0)
    ).astype(jnp.bfloat16)
    near_degree = jnp.sum(band_tiles.astype(jnp.float32), axis=1).reshape(frames)
    partner_rows = gathered.reshape(-1, 128, embed_width)[partners]
    own_rows = embeddings.reshape(tile_count, 128, embed_width)
    inner_prod = jnp.einsum(
        "tkje,tie->tkji", partner_rows, own_rows, preferred_element_type=jnp.float32
    )
    affinity = (
        jnp.exp(0.5 * (inner_prod / math.sqrt(embed_width)))
        * (levels.astype(jnp.float32) / 8.0)[:, :, None, None]
        / 128.0
    )
    affinity = affinity.astype(jnp.bfloat16)
    far_degree = jnp.sum(affinity.astype(jnp.float32), axis=(1, 2)).reshape(frames)
    norm_scale = 1.0 / jnp.sqrt(near_degree + far_degree)

    def squares(residual):
        return total_over_devices(jnp.sum(residual * residual, axis=1))

    solution = jnp.zeros((channels, frames), jnp.float32)
    residual = labels
    direction = labels
    first_norm = jnp.sum(residual * residual, axis=1)
    scale_band = band_gather(norm_scale)
    for iteration in range(ITERS):
        lifted = (norm_scale[None, :] * direction).astype(jnp.bfloat16)
        padded = with_halo(lifted, ((("band", "seq"), 1),), RADIUS)
        windows = jnp.stack(
            [padded[:, position * 128 : position * 128 + window] for position in range(tile_count)],
            axis=0,
        )
        near_term = jnp.einsum(
            "tcw,twa->cta", windows, band_tiles, preferred_element_type=jnp.float32
        ).reshape(channels, frames)
        if iteration == 0:
            lifted_band = (scale_band[:, None, :] * labels_band.astype(jnp.float32)).astype(jnp.bfloat16)
        else:
            lifted_band = band_gather(lifted)
        spread = jnp.transpose(lifted_band, (1, 0, 2)).reshape(channels, -1, 128)
        far_tiles = spread[:, partners]
        far_term = jnp.einsum(
            "ctkj,tkji->cti", far_tiles, affinity, preferred_element_type=jnp.float32
        ).reshape(channels, frames)
        image = direction - spread_rate * norm_scale[None, :] * (near_term + far_term)
        sums = [jnp.sum(direction * image, axis=1)]
        last = iteration == ITERS - 1
        if not last:
            sums += [jnp.sum(residual * image, axis=1), jnp.sum(image * image, axis=1)]
        if iteration == 0:
            sums.append(first_norm)
        totals = total_over_devices(jnp.stack(sums))
        curve = totals[0]
        if iteration == 0:
            norm_now = totals[-1]
        alpha = norm_now / curve
        solution = solution + alpha[:, None] * direction
        if not last:
            residual = residual - alpha[:, None] * image
            norm_next = norm_now - 2.0 * alpha * totals[1] + alpha * alpha * totals[2]
            direction = residual + (norm_next / norm_now)[:, None] * direction
            norm_now = norm_next
    return solution


def solution(mesh):
    placed = (
        P(None, ("band", "seq")),
        P(("band", "seq")),
        P(("band", "seq"), None),
        P(),
        P(("band", "seq"), None),
        P(("band", "seq"), None),
        P(("band", "seq"), None),
    )
    return jax.shard_map(
        on_device, mesh=mesh, in_specs=placed, out_specs=P(None, ("band", "seq")), check_vma=False
    )
```

```python
import math

import jax
import jax.numpy as jnp
from jax import lax
from jax.experimental import pallas as pl
from jax.experimental.pallas import tpu as pltpu
from jax.sharding import PartitionSpec as P

RADIUS = 64
ITERS = 3


decay_len = 16.0
spread_rate = 0.9


def with_halo(cells, sides, width):
    for axis, dim in sides:
        count = lax.axis_size(axis)
        ends = count - 1
        head = lax.slice_in_dim(cells, 0, width, axis=dim)
        tail = lax.slice_in_dim(cells, cells.shape[dim] - width, cells.shape[dim], axis=dim)
        cells = jnp.concatenate(
            [
                lax.ppermute(tail, axis, [(i, (i + 1) % count) for i in range(ends)]),
                cells,
                lax.ppermute(head, axis, [((i + 1) % count, i) for i in range(ends)]),
            ],
            axis=dim,
        )
    return cells


def total_over_devices(values):
    for axis in ("seq", "band"):
        count = lax.axis_size(axis)
        spread = jnp.broadcast_to(values[None], (count,) + values.shape)
        rows = lax.all_to_all(spread, axis, split_axis=0, concat_axis=0, tiled=True)
        values = jnp.sum(rows, axis=0)
    return values


def band_gather(block):
    count = lax.axis_size("band")
    spread = jnp.broadcast_to(block[None], (count,) + block.shape)
    return lax.all_to_all(spread, "band", split_axis=0, concat_axis=0, tiled=True)


SLOT_BLOCK = 32


def affinity_kernel(part_ref, lev_ref, own_ref, *refs):
    partner_refs = refs[:SLOT_BLOCK]
    aff_ref, deg_ref = refs[SLOT_BLOCK], refs[SLOT_BLOCK + 1]
    tile = pl.program_id(0)
    block = pl.program_id(1)
    own = own_ref[0]
    total = jnp.zeros((1, own.shape[0]), jnp.float32)
    for slot in range(SLOT_BLOCK):
        rows = partner_refs[slot][0]
        inner = lax.dot_general(
            rows, own, (((1,), (1,)), ((), ())), preferred_element_type=jnp.float32
        )
        level = lev_ref[tile, block * SLOT_BLOCK + slot].astype(jnp.float32)
        weight = (
            jnp.exp(0.5 * (inner / math.sqrt(own.shape[1]))) * (level / 8.0) / 128.0
        ).astype(jnp.bfloat16)
        aff_ref[0, slot] = weight
        total = total + jnp.sum(weight.astype(jnp.float32), axis=0, keepdims=True)
    deg_ref[0, 0] = total


def affinity_blocks(own_rows, group_rows, partners, levels):
    tiles, width, embed = own_rows.shape
    slots = partners.shape[1]
    blocks = slots // SLOT_BLOCK

    def partner_spec(slot):
        return pl.BlockSpec(
            (1, width, embed), lambda t, b, part, lev: (part[t, b * SLOT_BLOCK + slot], 0, 0)
        )

    grid_spec = pltpu.PrefetchScalarGridSpec(
        num_scalar_prefetch=2,
        grid=(tiles, blocks),
        in_specs=[pl.BlockSpec((1, width, embed), lambda t, b, part, lev: (t, 0, 0))]
        + [partner_spec(slot) for slot in range(SLOT_BLOCK)],
        out_specs=[
            pl.BlockSpec((1, SLOT_BLOCK, width, width), lambda t, b, part, lev: (t, b, 0, 0)),
            pl.BlockSpec((1, 1, 1, width), lambda t, b, part, lev: (t, b, 0, 0)),
        ],
    )
    affinity, degree = pl.pallas_call(
        affinity_kernel,
        grid_spec=grid_spec,
        out_shape=[
            jax.ShapeDtypeStruct((tiles, slots, width, width), jnp.bfloat16),
            jax.ShapeDtypeStruct((tiles, blocks, 1, width), jnp.float32),
        ],
    )(partners, levels, own_rows, *([group_rows] * SLOT_BLOCK))
    return affinity, jnp.sum(degree[:, :, 0, :], axis=1).reshape(-1)


def on_device(posteriors, seed_mask, frame_perm, lengths, embeddings, partners, levels):
    channels, frames = posteriors.shape
    band_count = lax.axis_size("band")
    groups = lax.axis_size("seq")
    tile_count = frames // 128
    seeded = posteriors * seed_mask.astype(jnp.bfloat16)[None, :]
    ordered = jnp.take(seeded, frame_perm[0], axis=1).reshape(
        channels, band_count, frames // band_count
    )
    arrived = lax.all_to_all(ordered, "band", split_axis=1, concat_axis=1, tiled=True)
    labels = arrived.reshape(channels, frames).astype(jnp.float32)
    device = lax.axis_index("band") * groups + lax.axis_index("seq")
    frame_total = frames * band_count * groups
    window = 128 + 2 * RADIUS
    global_at = device * frames - RADIUS + jnp.arange(frames + 2 * RADIUS, dtype=jnp.int32)
    utt_ends = jnp.cumsum(lengths)
    owner_seg = jnp.sum((utt_ends[None, :] <= global_at[:, None]).astype(jnp.int32), axis=1)
    inside = (global_at >= 0) & (global_at < frame_total)
    tile_off = (jnp.arange(tile_count, dtype=jnp.int32) * 128)[:, None, None]
    win_pos = tile_off + jnp.arange(window, dtype=jnp.int32)[None, :, None]
    row_pos = tile_off + RADIUS + jnp.arange(128, dtype=jnp.int32)[None, None, :]
    offset = jnp.abs(win_pos - row_pos)
    linked = (
        (offset >= 1)
        & (offset <= RADIUS)
        & (owner_seg[win_pos] == owner_seg[row_pos])
        & inside[win_pos]
    )
    band_tiles = jnp.where(
        linked, jnp.exp(-offset.astype(jnp.float32) / decay_len), jnp.float32(0.0)
    ).astype(jnp.bfloat16)
    near_degree = jnp.sum(band_tiles.astype(jnp.float32), axis=1).reshape(frames)
    gathered = lax.all_gather(embeddings, "band", axis=0, tiled=True)
    labels_band = band_gather(arrived.reshape(channels, frames))
    labels_band, gathered = lax.optimization_barrier((labels_band, gathered))
    embed_width = embeddings.shape[1]
    own_rows = embeddings.reshape(tile_count, 128, embed_width)
    affinity, far_degree = affinity_blocks(
        own_rows, gathered.reshape(-1, 128, embed_width), partners, levels
    )
    norm_scale = 1.0 / jnp.sqrt(near_degree + far_degree)

    def squares(residual):
        return total_over_devices(jnp.sum(residual * residual, axis=1))

    solution = jnp.zeros((channels, frames), jnp.float32)
    residual = labels
    direction = labels
    first_norm = jnp.sum(residual * residual, axis=1)
    scale_band = band_gather(norm_scale)
    for iteration in range(ITERS):
        lifted = (norm_scale[None, :] * direction).astype(jnp.bfloat16)
        padded = with_halo(lifted, ((("band", "seq"), 1),), RADIUS)
        windows = jnp.stack(
            [padded[:, position * 128 : position * 128 + window] for position in range(tile_count)],
            axis=0,
        )
        near_term = jnp.einsum(
            "tcw,twa->cta", windows, band_tiles, preferred_element_type=jnp.float32
        ).reshape(channels, frames)
        if iteration == 0:
            lifted_band = (scale_band[:, None, :] * labels_band.astype(jnp.float32)).astype(jnp.bfloat16)
        else:
            lifted_band = band_gather(lifted)
        spread = jnp.transpose(lifted_band, (1, 0, 2)).reshape(channels, -1, 128)
        far_tiles = spread[:, partners]
        far_term = jnp.einsum(
            "ctkj,tkji->cti", far_tiles, affinity, preferred_element_type=jnp.float32
        ).reshape(channels, frames)
        image = direction - spread_rate * norm_scale[None, :] * (near_term + far_term)
        sums = [jnp.sum(direction * image, axis=1)]
        last = iteration == ITERS - 1
        if not last:
            sums += [jnp.sum(residual * image, axis=1), jnp.sum(image * image, axis=1)]
        if iteration == 0:
            sums.append(first_norm)
        totals = total_over_devices(jnp.stack(sums))
        curve = totals[0]
        if iteration == 0:
            norm_now = totals[-1]
        alpha = norm_now / curve
        solution = solution + alpha[:, None] * direction
        if not last:
            residual = residual - alpha[:, None] * image
            norm_next = norm_now - 2.0 * alpha * totals[1] + alpha * alpha * totals[2]
            direction = residual + (norm_next / norm_now)[:, None] * direction
            norm_now = norm_next
    return solution


def solution(mesh):
    placed = (
        P(None, ("band", "seq")),
        P(("band", "seq")),
        P(("band", "seq"), None),
        P(),
        P(("band", "seq"), None),
        P(("band", "seq"), None),
        P(("band", "seq"), None),
    )
    return jax.shard_map(
        on_device, mesh=mesh, in_specs=placed, out_specs=P(None, ("band", "seq")), check_vma=False
    )
```
